32 devices in a mesh: row: 8 (over z, core), col: 4 (over y, x).
Axes of the slice: x: 2, y: 2, z: 4, core: 2. Of those that a mesh axis runs over, the one named last changes fastest.
Arguments:
- trunk_in: bfloat16 [1536, 8192], P('col', 'row'), may hold values from -24 to 24
- conv_weight: bfloat16 [5, 1536, 1536], P(None, 'col'), may hold values from -0.0625 to 0.0625
- conv_bias: float32 [1536], P('col'), may hold values from -3 to 3
- norm_gain: float32 [1536], replicated, may hold values from 0.1 to 1.9
- pair_proj: bfloat16 [64, 1536], replicated, may hold values from -0.15625 to 0.15625
- pair_in: bfloat16 [512, 128, 128], P('row', 'col'), may hold values from -6 to 6
- opm_weight: bfloat16 [1024, 128], replicated, may hold values from -0.1875 to 0.1875
- pair_bias: float32 [128], replicated, may hold values from -3 to 3
Outputs:
- trunk_out: bfloat16 [1536, 8192], P('col', 'row')
- pair_out: bfloat16 [512, 128, 128], P('row', 'col')
The draws below stay inside these ranges and needn't reach their ends.
All inputs are finite; a program needn't handle non-finite values.
Results may differ from the reference program's by a relative error of at most 0.012.
Values may be sent and summed in bfloat16 or wider, within the bound.
No kernel may reach another device: no remote copies, remote signals or barrier semaphores. Data moves between devices by JAX's collectives and lax.ppermute only.
A program may use at most 64 MiB of HBM per device.

```python
import math
import jax
import jax.numpy as jnp
from jax import lax

TRUNK_CHANNELS = 1536
KW = 5
DILATION_STEP = 8
POOL = 16
OPM = 32
PAIR = 128
TOTAL_TOKENS = 8192
PAIR_LEN = 128
PAIR_ROWS = 512
POOL_DEV = 64
N_ROW = 8


def draw_trunk_in(key, part):
    first, second, third = jax.random.split(key, 3)
    base = jax.random.truncated_normal(first, -4.0, 4.0, (TRUNK_CHANNELS, TOTAL_TOKENS), jnp.float32)
    row_scale = jnp.exp(jax.random.uniform(second, (1, TOTAL_TOKENS), jnp.float32, math.log(0.3), math.log(3.0)))
    col_scale = jnp.exp(jax.random.uniform(third, (TRUNK_CHANNELS, 1), jnp.float32, math.log(0.5), math.log(2.0)))
    return (base * row_scale * col_scale).astype(jnp.bfloat16)


def steps_of(rng, dims, cuts, low, largest):
    def one(dim, parts):
        draws = jax.random.uniform(jax.random.fold_in(jax.random.fold_in(rng, 6), dim), (parts,), jnp.float32, low / len(cuts), largest / len(cuts))
        return jnp.repeat(jnp.exp(draws), dims[dim] // parts).reshape((-1,) + (1,) * (len(dims) - dim - 1))

    gain = one(*cuts[0])
    for cut in cuts[1:]:
        gain = gain * one(*cut)
    return gain


def centred(own_key, shape, deviation, most, cuts=(), dtype=jnp.bfloat16):
    drawn = jax.random.normal(own_key, shape, jnp.float32) * deviation
    if len(cuts) > 0:
        drawn = steps_of(own_key, shape, cuts, -0.22, 0.18) * drawn
    return jnp.clip(drawn, min=-most, max=most).astype(dtype)


def setup_inputs(seed: int = 0) -> dict:
    splits = jax.random.split(jax.random.key(seed), 9)
    trunk_in = draw_trunk_in(jax.random.fold_in(splits[8], 71), 0)
    conv_weight = centred(splits[1], (KW, TRUNK_CHANNELS, TRUNK_CHANNELS), (KW * TRUNK_CHANNELS) ** -0.5, 0.0625, ((1, 4),))
    conv_bias = centred(splits[2], (TRUNK_CHANNELS,), 0.5, 3.0, ((0, 4),), jnp.float32)
    norm_gain = jnp.clip(1.0 + 0.18 * jax.random.normal(splits[3], (TRUNK_CHANNELS,), jnp.float32), 0.1, 1.9)
    pair_proj = centred(splits[4], (2 * OPM, TRUNK_CHANNELS), TRUNK_CHANNELS ** -0.5, 0.15625)
    pair_in = centred(splits[5], (PAIR_ROWS, PAIR_LEN, PAIR), 1.0, 6.0, ((0, 8), (1, 4)))
    opm_weight = centred(splits[6], (OPM * OPM, PAIR), (OPM * OPM) ** -0.5, 0.1875)
    pair_bias = centred(splits[7], (PAIR,), 0.5, 3.0, (), jnp.float32)
    return {"trunk_in": trunk_in, "conv_weight": conv_weight, "conv_bias": conv_bias, "norm_gain": norm_gain, "pair_proj": pair_proj, "pair_in": pair_in, "opm_weight": opm_weight, "pair_bias": pair_bias}


EPSILON = 1e-05

def reference(trunk_in, conv_weight, conv_bias, norm_gain, pair_proj, pair_in, opm_weight, pair_bias):
    source = trunk_in.astype(jnp.float32)
    scale = lax.rsqrt(lax.optimization_barrier(jnp.mean(source * source, axis=0, keepdims=True)) + EPSILON)
    gelu_output = jax.nn.gelu(source * norm_gain[:, None] * scale).astype(jnp.bfloat16)
    padded_trunk = jnp.pad(gelu_output, ((0, 0), (2 * DILATION_STEP, 2 * DILATION_STEP)))
    conv_sum = jnp.zeros((TRUNK_CHANNELS, TOTAL_TOKENS), jnp.float32)
    for tap_offset in range(KW):
        shifted_rows = padded_trunk[:, tap_offset * DILATION_STEP:tap_offset * DILATION_STEP + TOTAL_TOKENS]
        conv_sum = conv_sum + jnp.dot(conv_weight[tap_offset], shifted_rows, preferred_element_type=jnp.float32)
    trunk_out = (source + conv_sum + conv_bias[:, None]).astype(jnp.bfloat16)
    pooled = trunk_out.astype(jnp.float32).reshape(TRUNK_CHANNELS, TOTAL_TOKENS // POOL, POOL).mean(axis=2).astype(jnp.bfloat16)
    pooled_f = pooled.astype(jnp.float32)
    projected = lax.dot_general(pooled, pair_proj, (((0,), (1,)), ((), ())), preferred_element_type=jnp.float32)
    sides = (projected * lax.rsqrt(lax.optimization_barrier(jnp.sum(pooled_f * pooled_f, axis=0)) / TRUNK_CHANNELS + EPSILON)[:, None]).astype(jnp.bfloat16)
    row_side = sides[:, :OPM]
    col_side = sides[:, OPM:]

    def one_block(block_index):
        row_start = (block_index * POOL_DEV).astype(jnp.int32)
        row_block = lax.dynamic_slice_in_dim(row_side, row_start, POOL_DEV, 0)
        window_start = (row_start // PAIR_LEN * PAIR_LEN).astype(jnp.int32)
        window_cols = lax.dynamic_slice_in_dim(col_side, window_start, PAIR_LEN, 0)
        base_tile = lax.dynamic_slice_in_dim(pair_in, row_start, POOL_DEV, 0)
        outer = (row_block.astype(jnp.float32)[:, None, :, None] * window_cols.astype(jnp.float32)[None, :, None, :]).astype(jnp.bfloat16)
        outer = outer.reshape(POOL_DEV * PAIR_LEN, OPM * OPM)
        update = jnp.dot(outer, opm_weight, preferred_element_type=jnp.float32).reshape(POOL_DEV, PAIR_LEN, PAIR)
        return (base_tile.astype(jnp.float32) + update + pair_bias).astype(jnp.bfloat16)
    blocks = lax.map(one_block, jnp.arange(N_ROW).astype(jnp.int32))
    pair_out = blocks.reshape(PAIR_ROWS, PAIR_LEN, PAIR)
    return (trunk_out, pair_out)
```

```python
import jax
import jax.numpy as jnp
from jax import lax
from jax.sharding import PartitionSpec as P

TRUNK_CHANNELS = 1536
DILATION_STEP = 8
POOL = 16
OPM = 32

EPSILON = 1e-05


def with_halo(cells, sides, width):
    for axis, dim in sides:
        count = lax.axis_size(axis)
        ends = count - 1
        head = lax.slice_in_dim(cells, 0, width, axis=dim)
        tail = lax.slice_in_dim(cells, cells.shape[dim] - width, cells.shape[dim], axis=dim)
        cells = jnp.concatenate(
            [
                lax.ppermute(tail, axis, [(i, (i + 1) % count) for i in range(ends)]),
                cells,
                lax.ppermute(head, axis, [((i + 1) % count, i) for i in range(ends)]),
            ],
            axis=dim,
        )
    return cells


def partner_2(block, axis, bit):
    count = lax.axis_size(axis)
    route = []
    for low in range(count):
        high = low | 1 << bit
        if high != low and high < count:
            route += [(low, high), (high, low)]
    return lax.ppermute(block, axis, route)


def peer_of(index, step, count):
    if count & (count - 1) == 0:
        return index ^ step
    return (index + step) % count


def from_peer(block, axis, step):
    count = lax.axis_size(axis)
    if count & (count - 1) == 0:
        route = [(i, i ^ step) for i in range(count)]
    else:
        route = [((i + step) % count, i) for i in range(count)]
    return lax.ppermute(block, axis, route)


def per_device(
    trunk_in, conv_weight, conv_bias, norm_gain, pair_proj, pair_in, opm_weight, pair_bias
):
    local_channels = trunk_in.shape[0]
    token_positions = trunk_in.shape[1]
    kernel = conv_weight.shape[0]
    border_width = (kernel // 2) * DILATION_STEP
    n_col = lax.axis_size("col")
    row_index = lax.axis_index("row")
    col_index = lax.axis_index("col")

    padded_raw = with_halo(trunk_in, (("row", 1),), border_width)
    padded_f = padded_raw.astype(jnp.float32)
    own_squares = jnp.sum(padded_f * padded_f, axis=0)
    squares = own_squares
    for step in range(1, n_col):
        squares = squares + from_peer(own_squares, "col", step)
    scale = lax.rsqrt(squares / TRUNK_CHANNELS + EPSILON)[None, :]

    gains = norm_gain.reshape(n_col, local_channels)
    weights = conv_weight.reshape(kernel, local_channels, n_col, local_channels)

    def conv_part(raw, source):
        gain = lax.dynamic_index_in_dim(gains, source, 0, keepdims=False)
        act = jax.nn.gelu(raw.astype(jnp.float32) * gain[:, None] * scale).astype(jnp.bfloat16)
        taps = lax.dynamic_index_in_dim(weights, source, 2, keepdims=False)
        part = None
        for tap_offset in range(kernel):
            term = jnp.dot(
                taps[tap_offset],
                act[:, tap_offset * DILATION_STEP : tap_offset * DILATION_STEP + token_positions],
                preferred_element_type=jnp.float32,
            )
            part = term if part is None else part + term
        return part

    carried = conv_part(padded_raw, col_index)
    for step in range(1, n_col):
        carried = carried + conv_part(
            from_peer(padded_raw, "col", step), peer_of(col_index, step, n_col)
        )

    source = trunk_in.astype(jnp.float32)
    trunk_out = (source + carried + conv_bias[:, None]).astype(jnp.bfloat16)
    pooled = (
        trunk_out.astype(jnp.float32)
        .reshape(local_channels, token_positions // POOL, POOL)
        .mean(axis=2)
        .astype(jnp.bfloat16)
    )
    own_proj = lax.dynamic_slice_in_dim(pair_proj, col_index * local_channels, local_channels, 1)
    pooled_f = pooled.astype(jnp.float32)
    partial_proj = lax.dot_general(
        pooled, own_proj, (((0,), (1,)), ((), ())), preferred_element_type=jnp.float32
    )
    packed = jnp.concatenate(
        [partial_proj, jnp.sum(pooled_f * pooled_f, axis=0)[:, None]], axis=1
    )
    total = packed
    for step in range(1, n_col):
        total = total + from_peer(packed, "col", step)
    side_width = partial_proj.shape[1]
    projected = total[:, :side_width]
    sums = total[:, side_width]
    sides = (projected * lax.rsqrt(sums / TRUNK_CHANNELS + EPSILON)[:, None]).astype(jnp.bfloat16)
    row_side = sides[:, :OPM]
    collected = sides[:, OPM:]
    col_block = pair_in.shape[1]
    pooled_rows = row_side.shape[0]
    per_window = col_block * n_col // pooled_rows
    in_window = row_index % per_window
    for bit_num in range(per_window.bit_length() - 1):
        partner = partner_2(collected, "row", bit_num)
        upper_half = in_window // 2**bit_num % 2 == 1
        collected = jnp.where(
            upper_half,
            jnp.concatenate([partner, collected], axis=0),
            jnp.concatenate([collected, partner], axis=0),
        )
    own_cols = lax.dynamic_slice_in_dim(collected, col_index * col_block, col_block, 0)
    outer = (
        row_side.astype(jnp.float32)[:, None, :, None]
        * own_cols.astype(jnp.float32)[None, :, None, :]
    ).astype(jnp.bfloat16)
    outer = outer.reshape(pooled_rows * col_block, OPM * OPM)
    update = jnp.dot(outer, opm_weight, preferred_element_type=jnp.float32).reshape(pair_in.shape)
    pair_out = (pair_in.astype(jnp.float32) + update + pair_bias).astype(jnp.bfloat16)
    return (trunk_out, pair_out)


def solution(mesh):
    return jax.shard_map(
        per_device,
        mesh=mesh,
        in_specs=(
            P("col", "row"),
            P(None, "col", None),
            P("col"),
            P(),
            P(),
            P("row", "col", None),
            P(),
            P(),
        ),
        out_specs=(P("col", "row"), P("row", "col", None)),
        check_vma=False,
    )
```

```python
import jax
import jax.numpy as jnp
from jax import lax
from jax.sharding import PartitionSpec as P

TRUNK_CHANNELS = 1536
DILATION_STEP = 8
POOL = 16
OPM = 32

EPSILON = 1e-05


def with_halo(cells, sides, width):
    for axis, dim in sides:
        count = lax.axis_size(axis)
        ends = count - 1
        head = lax.slice_in_dim(cells, 0, width, axis=dim)
        tail = lax.slice_in_dim(cells, cells.shape[dim] - width, cells.shape[dim], axis=dim)
        cells = jnp.concatenate(
            [
                lax.ppermute(tail, axis, [(i, (i + 1) % count) for i in range(ends)]),
                cells,
                lax.ppermute(head, axis, [((i + 1) % count, i) for i in range(ends)]),
            ],
            axis=dim,
        )
    return cells


def partner_2(block, axis, bit):
    count = lax.axis_size(axis)
    route = []
    for low in range(count):
        high = low | 1 << bit
        if high != low and high < count:
            route += [(low, high), (high, low)]
    return lax.ppermute(block, axis, route)


def peer_of(index, step, count):
    if count & (count - 1) == 0:
        return index ^ step
    return (index + step) % count


def from_peer(block, axis, step):
    count = lax.axis_size(axis)
    if count & (count - 1) == 0:
        route = [(i, i ^ step) for i in range(count)]
    else:
        route = [((i + step) % count, i) for i in range(count)]
    return lax.ppermute(block, axis, route)


def per_device(
    trunk_in, conv_weight, conv_bias, norm_gain, pair_proj, pair_in, opm_weight, pair_bias
):
    local_channels = trunk_in.shape[0]
    token_positions = trunk_in.shape[1]
    kernel = conv_weight.shape[0]
    border_width = (kernel // 2) * DILATION_STEP
    n_col = lax.axis_size("col")
    row_index = lax.axis_index("row")
    col_index = lax.axis_index("col")

    source = trunk_in.astype(jnp.float32)
    own_squares = jnp.sum(source * source, axis=0)
    squares = own_squares
    for step in range(1, n_col):
        squares = squares + from_peer(own_squares, "col", step)
    scale = lax.rsqrt(squares / TRUNK_CHANNELS + EPSILON)[None, :]

    blocks = [trunk_in] + [from_peer(trunk_in, "col", step) for step in range(1, n_col)]
    stacked = jnp.stack(blocks)
    order = jnp.arange(n_col, dtype=jnp.int32)
    if n_col & (n_col - 1) == 0:
        order = jnp.bitwise_xor(order, col_index)
    else:
        order = (order - col_index) % n_col
    raw_full = jnp.take(stacked, order, axis=0).reshape(n_col * local_channels, token_positions)
    act = jax.nn.gelu(raw_full.astype(jnp.float32) * norm_gain[:, None] * scale).astype(
        jnp.bfloat16
    )
    padded = jnp.pad(act, ((0, 0), (border_width, border_width)))
    carried = None
    for tap_offset in range(kernel):
        term = jnp.dot(
            conv_weight[tap_offset],
            padded[:, tap_offset * DILATION_STEP : tap_offset * DILATION_STEP + token_positions],
            preferred_element_type=jnp.float32,
        )
        carried = term if carried is None else carried + term

    n_row = lax.axis_size("row")
    left = lax.ppermute(
        act[:, token_positions - border_width :], "row", [(i, i + 1) for i in range(n_row - 1)]
    )
    right = lax.ppermute(act[:, :border_width], "row", [(i + 1, i) for i in range(n_row - 1)])
    centre = kernel // 2
    left_fix = None
    right_fix = None
    for tap_offset in range(centre):
        reach = (centre - tap_offset) * DILATION_STEP
        term = jnp.dot(
            conv_weight[tap_offset],
            left[:, border_width - reach :],
            preferred_element_type=jnp.float32,
        )
        term = jnp.pad(term, ((0, 0), (0, border_width - reach)))
        left_fix = term if left_fix is None else left_fix + term
        far = kernel - 1 - tap_offset
        term = jnp.dot(
            conv_weight[far], right[:, :reach], preferred_element_type=jnp.float32
        )
        term = jnp.pad(term, ((0, 0), (border_width - reach, 0)))
        right_fix = term if right_fix is None else right_fix + term
    carried = carried + jnp.pad(left_fix, ((0, 0), (0, token_positions - border_width)))
    carried = carried + jnp.pad(right_fix, ((0, 0), (token_positions - border_width, 0)))

    trunk_out = (source + carried + conv_bias[:, None]).astype(jnp.bfloat16)
    pooled = (
        trunk_out.astype(jnp.float32)
        .reshape(local_channels, token_positions // POOL, POOL)
        .mean(axis=2)
        .astype(jnp.bfloat16)
    )
    own_proj = lax.dynamic_slice_in_dim(pair_proj, col_index * local_channels, local_channels, 1)
    pooled_f = pooled.astype(jnp.float32)
    partial_proj = lax.dot_general(
        pooled, own_proj, (((0,), (1,)), ((), ())), preferred_element_type=jnp.float32
    )
    packed = jnp.concatenate(
        [partial_proj, jnp.sum(pooled_f * pooled_f, axis=0)[:, None]], axis=1
    )
    total = packed
    for step in range(1, n_col):
        total = total + from_peer(packed, "col", step)
    side_width = partial_proj.shape[1]
    projected = total[:, :side_width]
    sums = total[:, side_width]
    sides = (projected * lax.rsqrt(sums / TRUNK_CHANNELS + EPSILON)[:, None]).astype(jnp.bfloat16)
    row_side = sides[:, :OPM]
    collected = sides[:, OPM:]
    col_block = pair_in.shape[1]
    pooled_rows = row_side.shape[0]
    per_window = col_block * n_col // pooled_rows
    in_window = row_index % per_window
    for bit_num in range(per_window.bit_length() - 1):
        partner = partner_2(collected, "row", bit_num)
        upper_half = in_window // 2**bit_num % 2 == 1
        collected = jnp.where(
            upper_half,
            jnp.concatenate([partner, collected], axis=0),
            jnp.concatenate([collected, partner], axis=0),
        )
    own_cols = lax.dynamic_slice_in_dim(collected, col_index * col_block, col_block, 0)
    outer = (
        row_side.astype(jnp.float32)[:, None, :, None]
        * own_cols.astype(jnp.float32)[None, :, None, :]
    ).astype(jnp.bfloat16)
    outer = outer.reshape(pooled_rows * col_block, OPM * OPM)
    update = jnp.dot(outer, opm_weight, preferred_element_type=jnp.float32).reshape(pair_in.shape)
    pair_out = (pair_in.astype(jnp.float32) + update + pair_bias).astype(jnp.bfloat16)
    return (trunk_out, pair_out)


def solution(mesh):
    return jax.shard_map(
        per_device,
        mesh=mesh,
        in_specs=(
            P("col", "row"),
            P(None, "col", None),
            P("col"),
            P(),
            P(),
            P("row", "col", None),
            P(),
            P(),
        ),
        out_specs=(P("col", "row"), P("row", "col", None)),
        check_vma=False,
    )
```

```python
import jax
import jax.numpy as jnp
from jax import lax
from jax.sharding import PartitionSpec as P

TRUNK_CHANNELS = 1536
DILATION_STEP = 8
POOL = 16
OPM = 32

EPSILON = 1e-05


def with_halo(cells, sides, width):
    for axis, dim in sides:
        count = lax.axis_size(axis)
        ends = count - 1
        head = lax.slice_in_dim(cells, 0, width, axis=dim)
        tail = lax.slice_in_dim(cells, cells.shape[dim] - width, cells.shape[dim], axis=dim)
        cells = jnp.concatenate(
            [
                lax.ppermute(tail, axis, [(i, (i + 1) % count) for i in range(ends)]),
                cells,
                lax.ppermute(head, axis, [((i + 1) % count, i) for i in range(ends)]),
            ],
            axis=dim,
        )
    return cells


def partner_2(block, axis, bit):
    count = lax.axis_size(axis)
    route = []
    for low in range(count):
        high = low | 1 << bit
        if high != low and high < count:
            route += [(low, high), (high, low)]
    return lax.ppermute(block, axis, route)


def peer_of(index, step, count):
    if count & (count - 1) == 0:
        return index ^ step
    return (index + step) % count


def from_peer(block, axis, step):
    count = lax.axis_size(axis)
    if count & (count - 1) == 0:
        route = [(i, i ^ step) for i in range(count)]
    else:
        route = [((i + step) % count, i) for i in range(count)]
    return lax.ppermute(block, axis, route)


def per_device(
    trunk_in, conv_weight, conv_bias, norm_gain, pair_proj, pair_in, opm_weight, pair_bias
):
    local_channels = trunk_in.shape[0]
    token_positions = trunk_in.shape[1]
    kernel = conv_weight.shape[0]
    border_width = (kernel // 2) * DILATION_STEP
    n_col = lax.axis_size("col")
    row_index = lax.axis_index("row")
    col_index = lax.axis_index("col")

    n_row = lax.axis_size("row")
    from_left = lax.ppermute(
        trunk_in[:, token_positions - border_width :], "row", [(i, i + 1) for i in range(n_row - 1)]
    )
    from_right = lax.ppermute(
        trunk_in[:, :border_width], "row", [(i + 1, i) for i in range(n_row - 1)]
    )
    cores = [from_peer(trunk_in, "col", step) for step in range(1, n_col)]
    own_edges = jnp.concatenate([from_left, from_right], axis=1)
    padded_own = jnp.concatenate([from_left, trunk_in, from_right], axis=1)
    padded_f = padded_own.astype(jnp.float32)
    own_squares = jnp.sum(padded_f * padded_f, axis=0)
    squares = own_squares
    for step in range(1, n_col):
        squares = squares + from_peer(own_squares, "col", step)
    scale = lax.rsqrt(squares / TRUNK_CHANNELS + EPSILON)[None, :]
    edges = [from_peer(own_edges, "col", step) for step in range(1, n_col)]

    gains = norm_gain.reshape(n_col, local_channels)
    padded = jnp.zeros((n_col * local_channels, token_positions + 2 * border_width), jnp.bfloat16)

    def place(padded, raw, source_index):
        gain = lax.dynamic_index_in_dim(gains, source_index, 0, keepdims=False)
        act = jax.nn.gelu(raw.astype(jnp.float32) * gain[:, None] * scale).astype(jnp.bfloat16)
        return lax.dynamic_update_slice(padded, act, (source_index * local_channels, 0))

    padded = place(padded, padded_own, col_index)
    for step in range(1, n_col):
        raw = jnp.concatenate(
            [edges[step - 1][:, :border_width], cores[step - 1], edges[step - 1][:, border_width:]],
            axis=1,
        )
        padded = place(padded, raw, peer_of(col_index, step, n_col))
    carried = None
    for tap_offset in range(kernel):
        term = jnp.dot(
            conv_weight[tap_offset],
            padded[:, tap_offset * DILATION_STEP : tap_offset * DILATION_STEP + token_positions],
            preferred_element_type=jnp.float32,
        )
        carried = term if carried is None else carried + term

    source = trunk_in.astype(jnp.float32)
    trunk_out = (source + carried + conv_bias[:, None]).astype(jnp.bfloat16)
    pooled = (
        trunk_out.astype(jnp.float32)
        .reshape(local_channels, token_positions // POOL, POOL)
        .mean(axis=2)
        .astype(jnp.bfloat16)
    )
    own_proj = lax.dynamic_slice_in_dim(pair_proj, col_index * local_channels, local_channels, 1)
    pooled_f = pooled.astype(jnp.float32)
    partial_proj = lax.dot_general(
        pooled, own_proj, (((0,), (1,)), ((), ())), preferred_element_type=jnp.float32
    )
    packed = jnp.concatenate(
        [partial_proj, jnp.sum(pooled_f * pooled_f, axis=0)[:, None]], axis=1
    )
    total = packed
    for step in range(1, n_col):
        total = total + from_peer(packed, "col", step)
    side_width = partial_proj.shape[1]
    projected = total[:, :side_width]
    sums = total[:, side_width]
    sides = (projected * lax.rsqrt(sums / TRUNK_CHANNELS + EPSILON)[:, None]).astype(jnp.bfloat16)
    row_side = sides[:, :OPM]
    collected = sides[:, OPM:]
    col_block = pair_in.shape[1]
    pooled_rows = row_side.shape[0]
    per_window = col_block * n_col // pooled_rows
    in_window = row_index % per_window
    for bit_num in range(per_window.bit_length() - 1):
        partner = partner_2(collected, "row", bit_num)
        upper_half = in_window // 2**bit_num % 2 == 1
        collected = jnp.where(
            upper_half,
            jnp.concatenate([partner, collected], axis=0),
            jnp.concatenate([collected, partner], axis=0),
        )
    own_cols = lax.dynamic_slice_in_dim(collected, col_index * col_block, col_block, 0)
    outer = (
        row_side.astype(jnp.float32)[:, None, :, None]
        * own_cols.astype(jnp.float32)[None, :, None, :]
    ).astype(jnp.bfloat16)
    outer = outer.reshape(pooled_rows * col_block, OPM * OPM)
    update = jnp.dot(outer, opm_weight, preferred_element_type=jnp.float32).reshape(pair_in.shape)
    pair_out = (pair_in.astype(jnp.float32) + update + pair_bias).astype(jnp.bfloat16)
    return (trunk_out, pair_out)


def solution(mesh):
    return jax.shard_map(
        per_device,
        mesh=mesh,
        in_specs=(
            P("col", "row"),
            P(None, "col", None),
            P("col"),
            P(),
            P(),
            P("row", "col", None),
            P(),
            P(),
        ),
        out_specs=(P("col", "row"), P("row", "col", None)),
        check_vma=False,
    )
```

```python
import jax
import jax.numpy as jnp
from jax import lax
from jax.sharding import PartitionSpec as P
from jax.experimental import pallas as pl
from jax.experimental.pallas import tpu as pltpu

TRUNK_CHANNELS = 1536
DILATION_STEP = 8
POOL = 16
OPM = 32

EPSILON = 1e-05


def with_halo(cells, sides, width):
    for axis, dim in sides:
        count = lax.axis_size(axis)
        ends = count - 1
        head = lax.slice_in_dim(cells, 0, width, axis=dim)
        tail = lax.slice_in_dim(cells, cells.shape[dim] - width, cells.shape[dim], axis=dim)
        cells = jnp.concatenate(
            [
                lax.ppermute(tail, axis, [(i, (i + 1) % count) for i in range(ends)]),
                cells,
                lax.ppermute(head, axis, [((i + 1) % count, i) for i in range(ends)]),
            ],
            axis=dim,
        )
    return cells


def partner_2(block, axis, bit):
    count = lax.axis_size(axis)
    route = []
    for low in range(count):
        high = low | 1 << bit
        if high != low and high < count:
            route += [(low, high), (high, low)]
    return lax.ppermute(block, axis, route)


def peer_of(index, step, count):
    if count & (count - 1) == 0:
        return index ^ step
    return (index + step) % count


def from_peer(block, axis, step):
    count = lax.axis_size(axis)
    if count & (count - 1) == 0:
        route = [(i, i ^ step) for i in range(count)]
    else:
        route = [((i + step) % count, i) for i in range(count)]
    return lax.ppermute(block, axis, route)


LANE = 128
SLAB = 256


def conv_kernel(n_src, kernel, local_channels, token_positions):
    def body(ids_ref, scale_ref, gain_ref, bias_ref, *refs):
        cores = refs[:n_src]
        edges = refs[n_src : 2 * n_src]
        w_hbm = refs[2 * n_src]
        out_ref, pooled_ref, act_ref, w_buf, acc_ref, sems = refs[2 * n_src + 1 :]
        copies = [
            pltpu.make_async_copy(w_hbm.at[tap], w_buf.at[tap], sems.at[tap])
            for tap in range(kernel)
        ]
        for copy in copies:
            copy.start()
        width = token_positions + 2 * LANE
        for s in range(n_src):
            row0 = pl.multiple_of(ids_ref[s] * local_channels, 8)
            gain = gain_ref[pl.ds(row0, local_channels), :]
            for lo in range(0, token_positions, SLAB):
                raw = cores[s][:, lo : lo + SLAB].astype(jnp.float32)
                scl = scale_ref[:, LANE + lo : LANE + lo + SLAB]
                act_ref[pl.ds(row0, local_channels), LANE + lo : LANE + lo + SLAB] = jax.nn.gelu(
                    raw * gain * scl
                )
            raw = edges[s][:, :LANE].astype(jnp.float32)
            act_ref[pl.ds(row0, local_channels), 0:LANE] = jax.nn.gelu(
                raw * gain * scale_ref[:, 0:LANE]
            )
            raw = edges[s][:, LANE:].astype(jnp.float32)
            act_ref[pl.ds(row0, local_channels), width - LANE : width] = jax.nn.gelu(
                raw * gain * scale_ref[:, width - LANE : width]
            )
        centre = kernel // 2
        for tap in range(kernel):
            copies[tap].wait()
            start = LANE + (tap - centre) * DILATION_STEP
            for lo in range(0, token_positions, SLAB):
                rhs = act_ref[:, start + lo : start + lo + SLAB].astype(jnp.bfloat16)
                term = jnp.dot(w_buf[tap], rhs, preferred_element_type=jnp.float32)
                if tap == 0:
                    acc_ref[:, lo : lo + SLAB] = term
                else:
                    acc_ref[:, lo : lo + SLAB] += term
        pool_rows = lax.broadcasted_iota(jnp.int32, (SLAB, SLAB // POOL), 0) // POOL
        pool_cols = lax.broadcasted_iota(jnp.int32, (SLAB, SLAB // POOL), 1)
        pool = jnp.where(pool_rows == pool_cols, 1.0 / POOL, 0.0).astype(jnp.bfloat16)
        for lo in range(0, token_positions, SLAB):
            out = (
                cores[0][:, lo : lo + SLAB].astype(jnp.float32)
                + acc_ref[:, lo : lo + SLAB]
                + bias_ref[...]
            ).astype(jnp.bfloat16)
            out_ref[:, lo : lo + SLAB] = out
            pooled_ref[:, lo // POOL : (lo + SLAB) // POOL] = jnp.dot(
                out, pool, preferred_element_type=jnp.float32
            )

    return body


def fused_conv(ids, scale_ext, gains, bias, cores, edges, weights):
    n_src = len(cores)
    kernel, local_channels, all_channels = weights.shape
    token_positions = cores[0].shape[1]
    width = token_positions + 2 * LANE
    vmem = pl.BlockSpec(memory_space=pltpu.VMEM)
    return pl.pallas_call(
        conv_kernel(n_src, kernel, local_channels, token_positions),
        out_shape=(
            jax.ShapeDtypeStruct((local_channels, token_positions), jnp.bfloat16),
            jax.ShapeDtypeStruct((local_channels, token_positions // POOL), jnp.float32),
        ),
        in_specs=[pl.BlockSpec(memory_space=pltpu.SMEM), vmem, vmem, vmem]
        + [vmem] * (2 * n_src)
        + [pl.BlockSpec(memory_space=pl.ANY)],
        out_specs=(vmem, vmem),
        scratch_shapes=[
            pltpu.VMEM((all_channels, width), jnp.float32),
            pltpu.VMEM((kernel, local_channels, all_channels), jnp.bfloat16),
            pltpu.VMEM((local_channels, token_positions), jnp.float32),
            pltpu.SemaphoreType.DMA((kernel,)),
        ],
        compiler_params=pltpu.CompilerParams(vmem_limit_bytes=60 * 1024 * 1024),
    )(ids, scale_ext, gains, bias, *cores, *edges, weights)


def per_device(
    trunk_in, conv_weight, conv_bias, norm_gain, pair_proj, pair_in, opm_weight, pair_bias
):
    local_channels = trunk_in.shape[0]
    token_positions = trunk_in.shape[1]
    kernel = conv_weight.shape[0]
    border_width = (kernel // 2) * DILATION_STEP
    n_col = lax.axis_size("col")
    row_index = lax.axis_index("row")
    col_index = lax.axis_index("col")

    n_row = lax.axis_size("row")
    from_left = lax.ppermute(
        trunk_in[:, token_positions - border_width :], "row", [(i, i + 1) for i in range(n_row - 1)]
    )
    from_right = lax.ppermute(
        trunk_in[:, :border_width], "row", [(i + 1, i) for i in range(n_row - 1)]
    )
    cores = [from_peer(trunk_in, "col", step) for step in range(1, n_col)]
    own_edges = jnp.concatenate([from_left, from_right], axis=1)
    padded_own = jnp.concatenate([from_left, trunk_in, from_right], axis=1)
    padded_f = padded_own.astype(jnp.float32)
    own_squares = jnp.sum(padded_f * padded_f, axis=0)
    squares = own_squares
    for step in range(1, n_col):
        squares = squares + from_peer(own_squares, "col", step)
    scale = lax.rsqrt(squares / TRUNK_CHANNELS + EPSILON)[None, :]
    edges = [from_peer(own_edges, "col", step) for step in range(1, n_col)]

    ids = jnp.stack([col_index] + [peer_of(col_index, step, n_col) for step in range(1, n_col)])
    ids = ids.astype(jnp.int32)
    pad = LANE - border_width
    scale_ext = jnp.pad(scale, ((0, 0), (pad, pad)), constant_values=1.0)

    def tiles(edge_pair):
        return jnp.concatenate(
            [
                jnp.pad(edge_pair[:, :border_width], ((0, 0), (pad, 0))),
                jnp.pad(edge_pair[:, border_width:], ((0, 0), (0, pad))),
            ],
            axis=1,
        )

    trunk_out, pooled_f = fused_conv(
        ids,
        scale_ext,
        norm_gain[:, None],
        conv_bias[:, None],
        [trunk_in] + cores,
        [tiles(own_edges)] + [tiles(edge) for edge in edges],
        conv_weight,
    )
    pooled = pooled_f.astype(jnp.bfloat16)
    own_proj = lax.dynamic_slice_in_dim(pair_proj, col_index * local_channels, local_channels, 1)
    pooled_f = pooled.astype(jnp.float32)
    partial_proj = lax.dot_general(
        pooled, own_proj, (((0,), (1,)), ((), ())), preferred_element_type=jnp.float32
    )
    packed = jnp.concatenate(
        [partial_proj, jnp.sum(pooled_f * pooled_f, axis=0)[:, None]], axis=1
    )
    total = packed
    for step in range(1, n_col):
        total = total + from_peer(packed, "col", step)
    side_width = partial_proj.shape[1]
    projected = total[:, :side_width]
    sums = total[:, side_width]
    sides = (projected * lax.rsqrt(sums / TRUNK_CHANNELS + EPSILON)[:, None]).astype(jnp.bfloat16)
    row_side = sides[:, :OPM]
    collected = sides[:, OPM:]
    col_block = pair_in.shape[1]
    pooled_rows = row_side.shape[0]
    per_window = col_block * n_col // pooled_rows
    in_window = row_index % per_window
    for bit_num in range(per_window.bit_length() - 1):
        partner = partner_2(collected, "row", bit_num)
        upper_half = in_window // 2**bit_num % 2 == 1
        collected = jnp.where(
            upper_half,
            jnp.concatenate([partner, collected], axis=0),
            jnp.concatenate([collected, partner], axis=0),
        )
    own_cols = lax.dynamic_slice_in_dim(collected, col_index * col_block, col_block, 0)
    outer = (
        row_side.astype(jnp.float32)[:, None, :, None]
        * own_cols.astype(jnp.float32)[None, :, None, :]
    ).astype(jnp.bfloat16)
    outer = outer.reshape(pooled_rows * col_block, OPM * OPM)
    update = jnp.dot(outer, opm_weight, preferred_element_type=jnp.float32).reshape(pair_in.shape)
    pair_out = (pair_in.astype(jnp.float32) + update + pair_bias).astype(jnp.bfloat16)
    return (trunk_out, pair_out)


def solution(mesh):
    return jax.shard_map(
        per_device,
        mesh=mesh,
        in_specs=(
            P("col", "row"),
            P(None, "col", None),
            P("col"),
            P(),
            P(),
            P("row", "col", None),
            P(),
            P(),
        ),
        out_specs=(P("col", "row"), P("row", "col", None)),
        check_vma=False,
    )
```

```python
import jax
import jax.numpy as jnp
from jax import lax
from jax.sharding import PartitionSpec as P
from jax.experimental import pallas as pl
from jax.experimental.pallas import tpu as pltpu

TRUNK_CHANNELS = 1536
DILATION_STEP = 8
POOL = 16
OPM = 32

EPSILON = 1e-05


def with_halo(cells, sides, width):
    for axis, dim in sides:
        count = lax.axis_size(axis)
        ends = count - 1
        head = lax.slice_in_dim(cells, 0, width, axis=dim)
        tail = lax.slice_in_dim(cells, cells.shape[dim] - width, cells.shape[dim], axis=dim)
        cells = jnp.concatenate(
            [
                lax.ppermute(tail, axis, [(i, (i + 1) % count) for i in range(ends)]),
                cells,
                lax.ppermute(head, axis, [((i + 1) % count, i) for i in range(ends)]),
            ],
            axis=dim,
        )
    return cells


def partner_2(block, axis, bit):
    count = lax.axis_size(axis)
    route = []
    for low in range(count):
        high = low | 1 << bit
        if high != low and high < count:
            route += [(low, high), (high, low)]
    return lax.ppermute(block, axis, route)


def peer_of(index, step, count):
    if count & (count - 1) == 0:
        return index ^ step
    return (index + step) % count


def from_peer(block, axis, step):
    count = lax.axis_size(axis)
    if count & (count - 1) == 0:
        route = [(i, i ^ step) for i in range(count)]
    else:
        route = [((i + step) % count, i) for i in range(count)]
    return lax.ppermute(block, axis, route)


LANE = 128
SLAB = 256


def conv_kernel(n_src, kernel, local_channels, token_positions):
    border = (kernel // 2) * DILATION_STEP

    def body(ids_ref, scale_ref, edge_scale_ref, gain_ref, bias_ref, *refs):
        cores = refs[:n_src]
        edges = refs[n_src : 2 * n_src]
        w_hbm = refs[2 * n_src]
        out_ref, pooled_ref, act_ref, w_buf, acc_ref, sems = refs[2 * n_src + 1 :]
        copies = [
            pltpu.make_async_copy(w_hbm.at[tap], w_buf.at[tap], sems.at[tap])
            for tap in range(kernel)
        ]
        for copy in copies:
            copy.start()
        width = token_positions + 2 * LANE
        for s in range(n_src):
            row0 = pl.multiple_of(ids_ref[s] * local_channels, 8)
            gain = gain_ref[pl.ds(row0, local_channels), :]
            for lo in range(0, token_positions, SLAB):
                raw = cores[s][:, lo : lo + SLAB].astype(jnp.float32)
                scl = scale_ref[:, LANE + lo : LANE + lo + SLAB]
                act_ref[pl.ds(row0, local_channels), LANE + lo : LANE + lo + SLAB] = jax.nn.gelu(
                    raw * gain * scl
                )
            edge = jax.nn.gelu(edges[s][...].astype(jnp.float32) * gain * edge_scale_ref[...])
            act_ref[pl.ds(row0, local_channels), LANE - border : LANE] = edge[:, :border]
            act_ref[pl.ds(row0, local_channels), LANE + token_positions : LANE + token_positions + border] = edge[:, border:]
        centre = kernel // 2
        for tap in range(kernel):
            copies[tap].wait()
            start = LANE + (tap - centre) * DILATION_STEP
            for lo in range(0, token_positions, SLAB):
                rhs = act_ref[:, start + lo : start + lo + SLAB].astype(jnp.bfloat16)
                term = jnp.dot(w_buf[tap], rhs, preferred_element_type=jnp.float32)
                if tap == 0:
                    acc_ref[:, lo : lo + SLAB] = term
                else:
                    acc_ref[:, lo : lo + SLAB] += term
        pool_rows = lax.broadcasted_iota(jnp.int32, (SLAB, SLAB // POOL), 0) // POOL
        pool_cols = lax.broadcasted_iota(jnp.int32, (SLAB, SLAB // POOL), 1)
        pool = jnp.where(pool_rows == pool_cols, 1.0 / POOL, 0.0).astype(jnp.bfloat16)
        for lo in range(0, token_positions, SLAB):
            out = (
                cores[0][:, lo : lo + SLAB].astype(jnp.float32)
                + acc_ref[:, lo : lo + SLAB]
                + bias_ref[...]
            ).astype(jnp.bfloat16)
            out_ref[:, lo : lo + SLAB] = out
            pooled_ref[:, lo // POOL : (lo + SLAB) // POOL] = jnp.dot(
                out, pool, preferred_element_type=jnp.float32
            )

    return body


def fused_conv(ids, scale_ext, edge_scale, gains, bias, cores, edges, weights):
    n_src = len(cores)
    kernel, local_channels, all_channels = weights.shape
    token_positions = cores[0].shape[1]
    width = token_positions + 2 * LANE
    vmem = pl.BlockSpec(memory_space=pltpu.VMEM)
    return pl.pallas_call(
        conv_kernel(n_src, kernel, local_channels, token_positions),
        out_shape=(
            jax.ShapeDtypeStruct((local_channels, token_positions), jnp.bfloat16),
            jax.ShapeDtypeStruct((local_channels, token_positions // POOL), jnp.float32),
        ),
        in_specs=[pl.BlockSpec(memory_space=pltpu.SMEM), vmem, vmem, vmem, vmem]
        + [vmem] * (2 * n_src)
        + [pl.BlockSpec(memory_space=pl.ANY)],
        out_specs=(vmem, vmem),
        scratch_shapes=[
            pltpu.VMEM((all_channels, width), jnp.float32),
            pltpu.VMEM((kernel, local_channels, all_channels), jnp.bfloat16),
            pltpu.VMEM((local_channels, token_positions), jnp.float32),
            pltpu.SemaphoreType.DMA((kernel,)),
        ],
        compiler_params=pltpu.CompilerParams(vmem_limit_bytes=60 * 1024 * 1024),
    )(ids, scale_ext, edge_scale, gains, bias, *cores, *edges, weights)


def per_device(
    trunk_in, conv_weight, conv_bias, norm_gain, pair_proj, pair_in, opm_weight, pair_bias
):
    local_channels = trunk_in.shape[0]
    token_positions = trunk_in.shape[1]
    kernel = conv_weight.shape[0]
    border_width = (kernel // 2) * DILATION_STEP
    n_col = lax.axis_size("col")
    row_index = lax.axis_index("row")
    col_index = lax.axis_index("col")

    n_row = lax.axis_size("row")
    from_left = lax.ppermute(
        trunk_in[:, token_positions - border_width :], "row", [(i, i + 1) for i in range(n_row - 1)]
    )
    from_right = lax.ppermute(
        trunk_in[:, :border_width], "row", [(i + 1, i) for i in range(n_row - 1)]
    )
    cores = [from_peer(trunk_in, "col", step) for step in range(1, n_col)]
    own_edges = jnp.concatenate([from_left, from_right], axis=1)
    padded_own = jnp.concatenate([from_left, trunk_in, from_right], axis=1)
    padded_f = padded_own.astype(jnp.float32)
    own_squares = jnp.sum(padded_f * padded_f, axis=0)
    squares = lax.psum(own_squares, "col")
    scale = lax.rsqrt(squares / TRUNK_CHANNELS + EPSILON)[None, :]
    edges = [from_peer(own_edges, "col", step) for step in range(1, n_col)]

    ids = jnp.stack([col_index] + [peer_of(col_index, step, n_col) for step in range(1, n_col)])
    ids = ids.astype(jnp.int32)
    pad = LANE - border_width
    scale_ext = jnp.pad(scale, ((0, 0), (pad, pad)), constant_values=1.0)

    edge_scale = jnp.concatenate(
        [scale[:, :border_width], scale[:, border_width + token_positions :]], axis=1
    )

    trunk_out, pooled_f = fused_conv(
        ids,
        scale_ext,
        edge_scale,
        norm_gain[:, None],
        conv_bias[:, None],
        [trunk_in] + cores,
        [own_edges] + edges,
        conv_weight,
    )
    pooled = pooled_f.astype(jnp.bfloat16)
    own_proj = lax.dynamic_slice_in_dim(pair_proj, col_index * local_channels, local_channels, 1)
    pooled_f = pooled.astype(jnp.float32)
    partial_proj = lax.dot_general(
        pooled, own_proj, (((0,), (1,)), ((), ())), preferred_element_type=jnp.float32
    )
    packed = jnp.concatenate(
        [partial_proj, jnp.sum(pooled_f * pooled_f, axis=0)[:, None]], axis=1
    )
    total = packed
    for step in range(1, n_col):
        total = total + from_peer(packed, "col", step)
    side_width = partial_proj.shape[1]
    projected = total[:, :side_width]
    sums = total[:, side_width]
    sides = (projected * lax.rsqrt(sums / TRUNK_CHANNELS + EPSILON)[:, None]).astype(jnp.bfloat16)
    row_side = sides[:, :OPM]
    collected = sides[:, OPM:]
    col_block = pair_in.shape[1]
    pooled_rows = row_side.shape[0]
    per_window = col_block * n_col // pooled_rows
    in_window = row_index % per_window
    for bit_num in range(per_window.bit_length() - 1):
        partner = partner_2(collected, "row", bit_num)
        upper_half = in_window // 2**bit_num % 2 == 1
        collected = jnp.where(
            upper_half,
            jnp.concatenate([partner, collected], axis=0),
            jnp.concatenate([collected, partner], axis=0),
        )
    own_cols = lax.dynamic_slice_in_dim(collected, col_index * col_block, col_block, 0)
    outer = (
        row_side.astype(jnp.float32)[:, None, :, None]
        * own_cols.astype(jnp.float32)[None, :, None, :]
    ).astype(jnp.bfloat16)
    outer = outer.reshape(pooled_rows * col_block, OPM * OPM)
    update = jnp.dot(outer, opm_weight, preferred_element_type=jnp.float32).reshape(pair_in.shape)
    pair_out = (pair_in.astype(jnp.float32) + update + pair_bias).astype(jnp.bfloat16)
    return (trunk_out, pair_out)


def solution(mesh):
    return jax.shard_map(
        per_device,
        mesh=mesh,
        in_specs=(
            P("col", "row"),
            P(None, "col", None),
            P("col"),
            P(),
            P(),
            P("row", "col", None),
            P(),
            P(),
        ),
        out_specs=(P("col", "row"), P("row", "col", None)),
        check_vma=False,
    )
```

```python
import jax
import jax.numpy as jnp
from jax import lax
from jax.sharding import PartitionSpec as P
from jax.experimental import pallas as pl
from jax.experimental.pallas import tpu as pltpu

TRUNK_CHANNELS = 1536
DILATION_STEP = 8
POOL = 16
OPM = 32

EPSILON = 1e-05


def with_halo(cells, sides, width):
    for axis, dim in sides:
        count = lax.axis_size(axis)
        ends = count - 1
        head = lax.slice_in_dim(cells, 0, width, axis=dim)
        tail = lax.slice_in_dim(cells, cells.shape[dim] - width, cells.shape[dim], axis=dim)
        cells = jnp.concatenate(
            [
                lax.ppermute(tail, axis, [(i, (i + 1) % count) for i in range(ends)]),
                cells,
                lax.ppermute(head, axis, [((i + 1) % count, i) for i in range(ends)]),
            ],
            axis=dim,
        )
    return cells


def partner_2(block, axis, bit):
    count = lax.axis_size(axis)
    route = []
    for low in range(count):
        high = low | 1 << bit
        if high != low and high < count:
            route += [(low, high), (high, low)]
    return lax.ppermute(block, axis, route)


def peer_of(index, step, count):
    if count & (count - 1) == 0:
        return index ^ step
    return (index + step) % count


def from_peer(block, axis, step):
    count = lax.axis_size(axis)
    if count & (count - 1) == 0:
        route = [(i, i ^ step) for i in range(count)]
    else:
        route = [((i + step) % count, i) for i in range(count)]
    return lax.ppermute(block, axis, route)


def from_diagonal(block, row_step, step):
    n_row = lax.axis_size("row")
    n_col = lax.axis_size("col")
    route = []
    for r in range(n_row):
        if 0 <= r - row_step < n_row:
            for c in range(n_col):
                route.append(((r - row_step) * n_col + peer_of(c, step, n_col), r * n_col + c))
    return lax.ppermute(block, ("row", "col"), route)


LANE = 128
SLAB = 256


def conv_kernel(n_src, kernel, local_channels, main_width, left_at, has_right, out_width):
    border = (kernel // 2) * DILATION_STEP

    def pieces(s, mains, lefts, rights):
        found = [(lefts[s], left_at, LANE - border, border)]
        for lo in range(0, main_width, SLAB):
            found.append((mains[s], lo, LANE + lo, min(SLAB, main_width - lo)))
        if has_right:
            found.append((rights[s], 0, LANE + main_width, border))
        return found

    def body(ids_ref, gain_ref, bias_ref, *refs):
        mains = refs[:n_src]
        lefts = refs[n_src : 2 * n_src]
        rights = refs[2 * n_src : 3 * n_src] if has_right else None
        rest = refs[3 * n_src :] if has_right else refs[2 * n_src :]
        resid_ref, w_hbm, out_ref, pooled_ref, act_ref, w_buf, acc_ref, sems = rest
        copies = [
            pltpu.make_async_copy(w_hbm.at[tap], w_buf.at[tap], sems.at[tap])
            for tap in range(kernel)
        ]
        for copy in copies:
            copy.start()
        layout = [pieces(s, mains, lefts, rights) for s in range(n_src)]
        scales = []
        for index in range(len(layout[0])):
            total = None
            for s in range(n_src):
                ref, at, _, width = layout[s][index]
                raw = ref[:, at : at + width].astype(jnp.float32)
                part = jnp.sum(raw * raw, axis=0, keepdims=True)
                total = part if total is None else total + part
            scales.append(lax.rsqrt(total / TRUNK_CHANNELS + EPSILON))
        for s in range(n_src):
            row0 = pl.multiple_of(ids_ref[s] * local_channels, 8)
            gain = gain_ref[pl.ds(row0, local_channels), :]
            for (ref, at, lane, width), scale in zip(layout[s], scales):
                raw = ref[:, at : at + width].astype(jnp.float32)
                act_ref[pl.ds(row0, local_channels), lane : lane + width] = jax.nn.gelu(
                    raw * gain * scale
                )
        for tap in range(kernel):
            copies[tap].wait()
            start = LANE + (tap - kernel // 2) * DILATION_STEP
            for lo in range(0, out_width, SLAB):
                rhs = act_ref[:, start + lo : start + lo + SLAB].astype(jnp.bfloat16)
                term = jnp.dot(w_buf[tap], rhs, preferred_element_type=jnp.float32)
                if tap == 0:
                    acc_ref[:, lo : lo + SLAB] = term
                else:
                    acc_ref[:, lo : lo + SLAB] += term
        pool_rows = lax.broadcasted_iota(jnp.int32, (SLAB, SLAB // POOL), 0) // POOL
        pool_cols = lax.broadcasted_iota(jnp.int32, (SLAB, SLAB // POOL), 1)
        pool = jnp.where(pool_rows == pool_cols, 1.0 / POOL, 0.0).astype(jnp.bfloat16)
        for lo in range(0, out_width, SLAB):
            out = (
                resid_ref[:, lo : lo + SLAB].astype(jnp.float32)
                + acc_ref[:, lo : lo + SLAB]
                + bias_ref[...]
            ).astype(jnp.bfloat16)
            out_ref[:, lo : lo + SLAB] = out
            pooled_ref[:, lo // POOL : (lo + SLAB) // POOL] = jnp.dot(
                out, pool, preferred_element_type=jnp.float32
            )

    return body


def fused_conv(ids, gains, bias, mains, lefts, left_at, rights, resid, weights):
    n_src = len(mains)
    kernel, local_channels, all_channels = weights.shape
    main_width = mains[0].shape[1]
    out_width = resid.shape[1]
    has_right = rights is not None
    vmem = pl.BlockSpec(memory_space=pltpu.VMEM)
    operands = list(mains) + list(lefts) + (list(rights) if has_right else [])
    return pl.pallas_call(
        conv_kernel(n_src, kernel, local_channels, main_width, left_at, has_right, out_width),
        out_shape=(
            jax.ShapeDtypeStruct((local_channels, out_width), jnp.bfloat16),
            jax.ShapeDtypeStruct((local_channels, out_width // POOL), jnp.float32),
        ),
        in_specs=[pl.BlockSpec(memory_space=pltpu.SMEM), vmem, vmem]
        + [vmem] * len(operands)
        + [vmem, pl.BlockSpec(memory_space=pl.ANY)],
        out_specs=(vmem, vmem),
        scratch_shapes=[
            pltpu.VMEM((all_channels, out_width + 2 * LANE), jnp.float32),
            pltpu.VMEM((kernel, local_channels, all_channels), jnp.bfloat16),
            pltpu.VMEM((local_channels, out_width), jnp.float32),
            pltpu.SemaphoreType.DMA((kernel,)),
        ],
        compiler_params=pltpu.CompilerParams(vmem_limit_bytes=60 * 1024 * 1024),
    )(ids, gains, bias, *operands, resid, weights)


def per_device(
    trunk_in, conv_weight, conv_bias, norm_gain, pair_proj, pair_in, opm_weight, pair_bias
):
    local_channels = trunk_in.shape[0]
    token_positions = trunk_in.shape[1]
    kernel = conv_weight.shape[0]
    border_width = (kernel // 2) * DILATION_STEP
    n_col = lax.axis_size("col")
    row_index = lax.axis_index("row")
    col_index = lax.axis_index("col")

    n_row = lax.axis_size("row")
    half = token_positions // 2
    first_width = half + border_width
    first = [trunk_in[:, :first_width]] + [
        from_peer(trunk_in[:, :first_width], "col", step) for step in range(1, n_col)
    ]
    tail = trunk_in[:, token_positions - border_width :]
    head = trunk_in[:, :border_width]
    lefts = [from_diagonal(tail, 1, step) for step in range(n_col)]
    rights = [from_diagonal(head, -1, step) for step in range(n_col)]
    first, lefts = lax.optimization_barrier((first, lefts))
    second_own, _ = lax.optimization_barrier((trunk_in[:, half:], first))
    second = [second_own] + [
        from_peer(second_own, "col", step) for step in range(1, n_col)
    ]
    second, rights = lax.optimization_barrier((second, rights))

    ids = jnp.stack([col_index] + [peer_of(col_index, step, n_col) for step in range(1, n_col)])
    ids = ids.astype(jnp.int32)
    gains = norm_gain[:, None]
    bias = conv_bias[:, None]
    out_a, pooled_a = fused_conv(
        ids, gains, bias, first, lefts, 0, None, trunk_in[:, :half], conv_weight
    )
    out_b, pooled_b = fused_conv(
        ids, gains, bias, second, first, half - border_width, rights, trunk_in[:, half:], conv_weight
    )
    trunk_out = jnp.concatenate([out_a, out_b], axis=1)
    pooled = jnp.concatenate([pooled_a, pooled_b], axis=1).astype(jnp.bfloat16)
    own_proj = lax.dynamic_slice_in_dim(pair_proj, col_index * local_channels, local_channels, 1)
    pooled_f = pooled.astype(jnp.float32)
    partial_proj = lax.dot_general(
        pooled, own_proj, (((0,), (1,)), ((), ())), preferred_element_type=jnp.float32
    )
    packed = jnp.concatenate(
        [partial_proj, jnp.sum(pooled_f * pooled_f, axis=0)[:, None]], axis=1
    )
    total = packed
    for step in range(1, n_col):
        total = total + from_peer(packed, "col", step)
    side_width = partial_proj.shape[1]
    projected = total[:, :side_width]
    sums = total[:, side_width]
    sides = (projected * lax.rsqrt(sums / TRUNK_CHANNELS + EPSILON)[:, None]).astype(jnp.bfloat16)
    row_side = sides[:, :OPM]
    collected = sides[:, OPM:]
    col_block = pair_in.shape[1]
    pooled_rows = row_side.shape[0]
    per_window = col_block * n_col // pooled_rows
    in_window = row_index % per_window
    for bit_num in range(per_window.bit_length() - 1):
        partner = partner_2(collected, "row", bit_num)
        upper_half = in_window // 2**bit_num % 2 == 1
        collected = jnp.where(
            upper_half,
            jnp.concatenate([partner, collected], axis=0),
            jnp.concatenate([collected, partner], axis=0),
        )
    own_cols = lax.dynamic_slice_in_dim(collected, col_index * col_block, col_block, 0)
    outer = (
        row_side.astype(jnp.float32)[:, None, :, None]
        * own_cols.astype(jnp.float32)[None, :, None, :]
    ).astype(jnp.bfloat16)
    outer = outer.reshape(pooled_rows * col_block, OPM * OPM)
    update = jnp.dot(outer, opm_weight, preferred_element_type=jnp.float32).reshape(pair_in.shape)
    pair_out = (pair_in.astype(jnp.float32) + update + pair_bias).astype(jnp.bfloat16)
    return (trunk_out, pair_out)


def solution(mesh):
    return jax.shard_map(
        per_device,
        mesh=mesh,
        in_specs=(
            P("col", "row"),
            P(None, "col", None),
            P("col"),
            P(),
            P(),
            P("row", "col", None),
            P(),
            P(),
        ),
        out_specs=(P("col", "row"), P("row", "col", None)),
        check_vma=False,
    )
```

```python
import jax
import jax.numpy as jnp
from jax import lax
from jax.sharding import PartitionSpec as P
from jax.experimental import pallas as pl
from jax.experimental.pallas import tpu as pltpu

TRUNK_CHANNELS = 1536
DILATION_STEP = 8
POOL = 16
OPM = 32

EPSILON = 1e-05


def with_halo(cells, sides, width):
    for axis, dim in sides:
        count = lax.axis_size(axis)
        ends = count - 1
        head = lax.slice_in_dim(cells, 0, width, axis=dim)
        tail = lax.slice_in_dim(cells, cells.shape[dim] - width, cells.shape[dim], axis=dim)
        cells = jnp.concatenate(
            [
                lax.ppermute(tail, axis, [(i, (i + 1) % count) for i in range(ends)]),
                cells,
                lax.ppermute(head, axis, [((i + 1) % count, i) for i in range(ends)]),
            ],
            axis=dim,
        )
    return cells


def partner_2(block, axis, bit):
    count = lax.axis_size(axis)
    route = []
    for low in range(count):
        high = low | 1 << bit
        if high != low and high < count:
            route += [(low, high), (high, low)]
    return lax.ppermute(block, axis, route)


def peer_of(index, step, count):
    if count & (count - 1) == 0:
        return index ^ step
    return (index + step) % count


def from_peer(block, axis, step):
    count = lax.axis_size(axis)
    if count & (count - 1) == 0:
        route = [(i, i ^ step) for i in range(count)]
    else:
        route = [((i + step) % count, i) for i in range(count)]
    return lax.ppermute(block, axis, route)


LANE = 128
SLAB = 256


def conv_kernel(n_src, kernel, local_channels, token_positions):
    border = (kernel // 2) * DILATION_STEP

    def body(ids_ref, gain_ref, bias_ref, *refs):
        cores = refs[:n_src]
        edges = refs[n_src : 2 * n_src]
        w_hbm = refs[2 * n_src]
        out_ref, pooled_ref, act_ref, w_buf, acc_ref, sems = refs[2 * n_src + 1 :]
        copies = [
            pltpu.make_async_copy(w_hbm.at[tap], w_buf.at[tap], sems.at[tap])
            for tap in range(kernel)
        ]
        for copy in copies:
            copy.start()
        core_scales = []
        for lo in range(0, token_positions, SLAB):
            total = None
            for s in range(n_src):
                raw = cores[s][:, lo : lo + SLAB].astype(jnp.float32)
                part = jnp.sum(raw * raw, axis=0, keepdims=True)
                total = part if total is None else total + part
            core_scales.append(lax.rsqrt(total / TRUNK_CHANNELS + EPSILON))
        total = None
        for s in range(n_src):
            raw = edges[s][...].astype(jnp.float32)
            part = jnp.sum(raw * raw, axis=0, keepdims=True)
            total = part if total is None else total + part
        edge_scale = lax.rsqrt(total / TRUNK_CHANNELS + EPSILON)
        for s in range(n_src):
            row0 = pl.multiple_of(ids_ref[s] * local_channels, 8)
            gain = gain_ref[pl.ds(row0, local_channels), :]
            for lo, scl in zip(range(0, token_positions, SLAB), core_scales):
                raw = cores[s][:, lo : lo + SLAB].astype(jnp.float32)
                act_ref[pl.ds(row0, local_channels), LANE + lo : LANE + lo + SLAB] = jax.nn.gelu(
                    raw * gain * scl
                )
            edge = jax.nn.gelu(edges[s][...].astype(jnp.float32) * gain * edge_scale)
            act_ref[pl.ds(row0, local_channels), LANE - border : LANE] = edge[:, :border]
            act_ref[pl.ds(row0, local_channels), LANE + token_positions : LANE + token_positions + border] = edge[:, border:]
        centre = kernel // 2
        for tap in range(kernel):
            copies[tap].wait()
            start = LANE + (tap - centre) * DILATION_STEP
            for lo in range(0, token_positions, SLAB):
                rhs = act_ref[:, start + lo : start + lo + SLAB].astype(jnp.bfloat16)
                term = jnp.dot(w_buf[tap], rhs, preferred_element_type=jnp.float32)
                if tap == 0:
                    acc_ref[:, lo : lo + SLAB] = term
                else:
                    acc_ref[:, lo : lo + SLAB] += term
        pool_rows = lax.broadcasted_iota(jnp.int32, (SLAB, SLAB // POOL), 0) // POOL
        pool_cols = lax.broadcasted_iota(jnp.int32, (SLAB, SLAB // POOL), 1)
        pool = jnp.where(pool_rows == pool_cols, 1.0 / POOL, 0.0).astype(jnp.bfloat16)
        for lo in range(0, token_positions, SLAB):
            out = (
                cores[0][:, lo : lo + SLAB].astype(jnp.float32)
                + acc_ref[:, lo : lo + SLAB]
                + bias_ref[...]
            ).astype(jnp.bfloat16)
            out_ref[:, lo : lo + SLAB] = out
            pooled_ref[:, lo // POOL : (lo + SLAB) // POOL] = jnp.dot(
                out, pool, preferred_element_type=jnp.float32
            )

    return body


def fused_conv(ids, gains, bias, cores, edges, weights):
    n_src = len(cores)
    kernel, local_channels, all_channels = weights.shape
    token_positions = cores[0].shape[1]
    width = token_positions + 2 * LANE
    vmem = pl.BlockSpec(memory_space=pltpu.VMEM)
    return pl.pallas_call(
        conv_kernel(n_src, kernel, local_channels, token_positions),
        out_shape=(
            jax.ShapeDtypeStruct((local_channels, token_positions), jnp.bfloat16),
            jax.ShapeDtypeStruct((local_channels, token_positions // POOL), jnp.float32),
        ),
        in_specs=[pl.BlockSpec(memory_space=pltpu.SMEM), vmem, vmem]
        + [vmem] * (2 * n_src)
        + [pl.BlockSpec(memory_space=pl.ANY)],
        out_specs=(vmem, vmem),
        scratch_shapes=[
            pltpu.VMEM((all_channels, width), jnp.float32),
            pltpu.VMEM((kernel, local_channels, all_channels), jnp.bfloat16),
            pltpu.VMEM((local_channels, token_positions), jnp.float32),
            pltpu.SemaphoreType.DMA((kernel,)),
        ],
        compiler_params=pltpu.CompilerParams(vmem_limit_bytes=60 * 1024 * 1024),
    )(ids, gains, bias, *cores, *edges, weights)


def per_device(
    trunk_in, conv_weight, conv_bias, norm_gain, pair_proj, pair_in, opm_weight, pair_bias
):
    local_channels = trunk_in.shape[0]
    token_positions = trunk_in.shape[1]
    kernel = conv_weight.shape[0]
    border_width = (kernel // 2) * DILATION_STEP
    n_col = lax.axis_size("col")
    row_index = lax.axis_index("row")
    col_index = lax.axis_index("col")

    n_row = lax.axis_size("row")
    from_left = lax.ppermute(
        trunk_in[:, token_positions - border_width :], "row", [(i, i + 1) for i in range(n_row - 1)]
    )
    from_right = lax.ppermute(
        trunk_in[:, :border_width], "row", [(i + 1, i) for i in range(n_row - 1)]
    )
    cores = [from_peer(trunk_in, "col", step) for step in range(1, n_col)]
    own_edges = jnp.concatenate([from_left, from_right], axis=1)
    edges = [from_peer(own_edges, "col", step) for step in range(1, n_col)]

    ids = jnp.stack([col_index] + [peer_of(col_index, step, n_col) for step in range(1, n_col)])
    ids = ids.astype(jnp.int32)
    trunk_out, pooled_f = fused_conv(
        ids,
        norm_gain[:, None],
        conv_bias[:, None],
        [trunk_in] + cores,
        [own_edges] + edges,
        conv_weight,
    )
    pooled = pooled_f.astype(jnp.bfloat16)
    own_proj = lax.dynamic_slice_in_dim(pair_proj, col_index * local_channels, local_channels, 1)
    pooled_f = pooled.astype(jnp.float32)
    partial_proj = lax.dot_general(
        pooled, own_proj, (((0,), (1,)), ((), ())), preferred_element_type=jnp.float32
    )
    packed = jnp.concatenate(
        [partial_proj, jnp.sum(pooled_f * pooled_f, axis=0)[:, None]], axis=1
    )
    total = packed
    for step in range(1, n_col):
        total = total + from_peer(packed, "col", step)
    side_width = partial_proj.shape[1]
    projected = total[:, :side_width]
    sums = total[:, side_width]
    sides = (projected * lax.rsqrt(sums / TRUNK_CHANNELS + EPSILON)[:, None]).astype(jnp.bfloat16)
    row_side = sides[:, :OPM]
    collected = sides[:, OPM:]
    col_block = pair_in.shape[1]
    pooled_rows = row_side.shape[0]
    per_window = col_block * n_col // pooled_rows
    in_window = row_index % per_window
    for bit_num in range(per_window.bit_length() - 1):
        partner = partner_2(collected, "row", bit_num)
        upper_half = in_window // 2**bit_num % 2 == 1
        collected = jnp.where(
            upper_half,
            jnp.concatenate([partner, collected], axis=0),
            jnp.concatenate([collected, partner], axis=0),
        )
    own_cols = lax.dynamic_slice_in_dim(collected, col_index * col_block, col_block, 0)
    outer = (
        row_side.astype(jnp.float32)[:, None, :, None]
        * own_cols.astype(jnp.float32)[None, :, None, :]
    ).astype(jnp.bfloat16)
    outer = outer.reshape(pooled_rows * col_block, OPM * OPM)
    update = jnp.dot(outer, opm_weight, preferred_element_type=jnp.float32).reshape(pair_in.shape)
    pair_out = (pair_in.astype(jnp.float32) + update + pair_bias).astype(jnp.bfloat16)
    return (trunk_out, pair_out)


def solution(mesh):
    return jax.shard_map(
        per_device,
        mesh=mesh,
        in_specs=(
            P("col", "row"),
            P(None, "col", None),
            P("col"),
            P(),
            P(),
            P("row", "col", None),
            P(),
            P(),
        ),
        out_specs=(P("col", "row"), P("row", "col", None)),
        check_vma=False,
    )
```

```python
import jax
import jax.numpy as jnp
from jax import lax
from jax.sharding import PartitionSpec as P
from jax.experimental import pallas as pl
from jax.experimental.pallas import tpu as pltpu

TRUNK_CHANNELS = 1536
DILATION_STEP = 8
POOL = 16
OPM = 32

EPSILON = 1e-05


def with_halo(cells, sides, width):
    for axis, dim in sides:
        count = lax.axis_size(axis)
        ends = count - 1
        head = lax.slice_in_dim(cells, 0, width, axis=dim)
        tail = lax.slice_in_dim(cells, cells.shape[dim] - width, cells.shape[dim], axis=dim)
        cells = jnp.concatenate(
            [
                lax.ppermute(tail, axis, [(i, (i + 1) % count) for i in range(ends)]),
                cells,
                lax.ppermute(head, axis, [((i + 1) % count, i) for i in range(ends)]),
            ],
            axis=dim,
        )
    return cells


def partner_2(block, axis, bit):
    count = lax.axis_size(axis)
    route = []
    for low in range(count):
        high = low | 1 << bit
        if high != low and high < count:
            route += [(low, high), (high, low)]
    return lax.ppermute(block, axis, route)


def peer_of(index, step, count):
    if count & (count - 1) == 0:
        return index ^ step
    return (index + step) % count


def from_peer(block, axis, step):
    count = lax.axis_size(axis)
    if count & (count - 1) == 0:
        route = [(i, i ^ step) for i in range(count)]
    else:
        route = [((i + step) % count, i) for i in range(count)]
    return lax.ppermute(block, axis, route)


LANE = 128
SLAB = 256


def conv_kernel(n_src, kernel, local_channels, token_positions):
    border = (kernel // 2) * DILATION_STEP

    def body(ids_ref, gain_ref, bias_ref, proj_ref, *refs):
        core_hbm = refs[:n_src]
        edge_hbm = refs[n_src : 2 * n_src]
        w_hbm = refs[2 * n_src]
        (out_ref, side_ref, act_ref, w_buf, acc_ref, core_buf, edge_buf, pooled_buf, sems,
         in_sems) = refs[2 * n_src + 1 :]
        inputs = [
            pltpu.make_async_copy(core_hbm[s], core_buf.at[s], in_sems.at[s]) for s in range(n_src)
        ] + [
            pltpu.make_async_copy(edge_hbm[s], edge_buf.at[s], in_sems.at[n_src + s])
            for s in range(n_src)
        ]
        for copy in inputs:
            copy.start()
        copies = [
            pltpu.make_async_copy(w_hbm.at[tap], w_buf.at[tap], sems.at[tap])
            for tap in range(kernel)
        ]
        for copy in copies:
            copy.start()
        for copy in inputs:
            copy.wait()
        cores = [core_buf.at[s] for s in range(n_src)]
        edges = [edge_buf.at[s] for s in range(n_src)]
        core_scales = []
        for lo in range(0, token_positions, SLAB):
            total = None
            for s in range(n_src):
                raw = cores[s][:, lo : lo + SLAB].astype(jnp.float32)
                part = jnp.sum(raw * raw, axis=0, keepdims=True)
                total = part if total is None else total + part
            core_scales.append(lax.rsqrt(total / TRUNK_CHANNELS + EPSILON))
        total = None
        for s in range(n_src):
            raw = edges[s][...].astype(jnp.float32)
            part = jnp.sum(raw * raw, axis=0, keepdims=True)
            total = part if total is None else total + part
        edge_scale = lax.rsqrt(total / TRUNK_CHANNELS + EPSILON)
        for s in range(n_src):
            row0 = pl.multiple_of(ids_ref[s] * local_channels, 8)
            gain = gain_ref[pl.ds(row0, local_channels), :]
            for lo, scl in zip(range(0, token_positions, SLAB), core_scales):
                raw = cores[s][:, lo : lo + SLAB].astype(jnp.float32)
                act_ref[pl.ds(row0, local_channels), LANE + lo : LANE + lo + SLAB] = jax.nn.gelu(
                    raw * gain * scl
                )
            edge = jax.nn.gelu(edges[s][...].astype(jnp.float32) * gain * edge_scale)
            act_ref[pl.ds(row0, local_channels), LANE - border : LANE] = edge[:, :border]
            act_ref[pl.ds(row0, local_channels), LANE + token_positions : LANE + token_positions + border] = edge[:, border:]
        centre = kernel // 2
        for tap in range(kernel):
            copies[tap].wait()
            start = LANE + (tap - centre) * DILATION_STEP
            for lo in range(0, token_positions, SLAB):
                rhs = act_ref[:, start + lo : start + lo + SLAB].astype(jnp.bfloat16)
                term = jnp.dot(w_buf[tap], rhs, preferred_element_type=jnp.float32)
                if tap == 0:
                    acc_ref[:, lo : lo + SLAB] = term
                else:
                    acc_ref[:, lo : lo + SLAB] += term
        pool_rows = lax.broadcasted_iota(jnp.int32, (SLAB, SLAB // POOL), 0) // POOL
        pool_cols = lax.broadcasted_iota(jnp.int32, (SLAB, SLAB // POOL), 1)
        pool = jnp.where(pool_rows == pool_cols, 1.0 / POOL, 0.0).astype(jnp.bfloat16)
        for lo in range(0, token_positions, SLAB):
            out = (
                cores[0][:, lo : lo + SLAB].astype(jnp.float32)
                + acc_ref[:, lo : lo + SLAB]
                + bias_ref[...]
            ).astype(jnp.bfloat16)
            out_ref[:, lo : lo + SLAB] = out
            pooled_buf[:, lo // POOL : (lo + SLAB) // POOL] = jnp.dot(
                out, pool, preferred_element_type=jnp.float32
            )
        pooled = pooled_buf[...].astype(jnp.bfloat16)
        side_ref[: proj_ref.shape[0], :] = jnp.dot(
            proj_ref[...], pooled, preferred_element_type=jnp.float32
        )
        pooled_f = pooled.astype(jnp.float32)
        side_ref[proj_ref.shape[0] :, :] = jnp.sum(pooled_f * pooled_f, axis=0, keepdims=True)

    return body


def fused_conv(ids, gains, bias, own_proj, cores, edges, weights):
    n_src = len(cores)
    kernel, local_channels, all_channels = weights.shape
    token_positions = cores[0].shape[1]
    width = token_positions + 2 * LANE
    sides = own_proj.shape[0]
    vmem = pl.BlockSpec(memory_space=pltpu.VMEM)
    anywhere = pl.BlockSpec(memory_space=pl.ANY)
    return pl.pallas_call(
        conv_kernel(n_src, kernel, local_channels, token_positions),
        out_shape=(
            jax.ShapeDtypeStruct((local_channels, token_positions), jnp.bfloat16),
            jax.ShapeDtypeStruct((sides + 1, token_positions // POOL), jnp.float32),
        ),
        in_specs=[pl.BlockSpec(memory_space=pltpu.SMEM), vmem, vmem, vmem]
        + [anywhere] * (2 * n_src + 1),
        out_specs=(vmem, vmem),
        scratch_shapes=[
            pltpu.VMEM((all_channels, width), jnp.float32),
            pltpu.VMEM((kernel, local_channels, all_channels), jnp.bfloat16),
            pltpu.VMEM((local_channels, token_positions), jnp.float32),
            pltpu.VMEM((n_src, local_channels, token_positions), jnp.bfloat16),
            pltpu.VMEM((n_src,) + edges[0].shape, jnp.bfloat16),
            pltpu.VMEM((local_channels, token_positions // POOL), jnp.float32),
            pltpu.SemaphoreType.DMA((kernel,)),
            pltpu.SemaphoreType.DMA((2 * n_src,)),
        ],
        compiler_params=pltpu.CompilerParams(vmem_limit_bytes=60 * 1024 * 1024),
    )(ids, gains, bias, own_proj, *cores, *edges, weights)


def per_device(
    trunk_in, conv_weight, conv_bias, norm_gain, pair_proj, pair_in, opm_weight, pair_bias
):
    local_channels = trunk_in.shape[0]
    token_positions = trunk_in.shape[1]
    kernel = conv_weight.shape[0]
    border_width = (kernel // 2) * DILATION_STEP
    n_col = lax.axis_size("col")
    row_index = lax.axis_index("row")
    col_index = lax.axis_index("col")

    n_row = lax.axis_size("row")
    from_left = lax.ppermute(
        trunk_in[:, token_positions - border_width :], "row", [(i, i + 1) for i in range(n_row - 1)]
    )
    from_right = lax.ppermute(
        trunk_in[:, :border_width], "row", [(i + 1, i) for i in range(n_row - 1)]
    )
    cores = [from_peer(trunk_in, "col", step) for step in range(1, n_col)]
    own_edges = jnp.concatenate([from_left, from_right], axis=1)
    edges = [from_peer(own_edges, "col", step) for step in range(1, n_col)]

    ids = jnp.stack([col_index] + [peer_of(col_index, step, n_col) for step in range(1, n_col)])
    ids = ids.astype(jnp.int32)
    own_proj = lax.dynamic_slice_in_dim(pair_proj, col_index * local_channels, local_channels, 1)
    trunk_out, packed = fused_conv(
        ids,
        norm_gain[:, None],
        conv_bias[:, None],
        own_proj,
        [trunk_in] + cores,
        [own_edges] + edges,
        conv_weight,
    )
    total = packed
    for step in range(1, n_col):
        total = total + from_peer(packed, "col", step)
    total = total.T
    side_width = total.shape[1] - 1
    projected = total[:, :side_width]
    sums = total[:, side_width]
    sides = (projected * lax.rsqrt(sums / TRUNK_CHANNELS + EPSILON)[:, None]).astype(jnp.bfloat16)
    row_side = sides[:, :OPM]
    collected = sides[:, OPM:]
    col_block = pair_in.shape[1]
    pooled_rows = row_side.shape[0]
    per_window = col_block * n_col // pooled_rows
    in_window = row_index % per_window
    for bit_num in range(per_window.bit_length() - 1):
        partner = partner_2(collected, "row", bit_num)
        upper_half = in_window // 2**bit_num % 2 == 1
        collected = jnp.where(
            upper_half,
            jnp.concatenate([partner, collected], axis=0),
            jnp.concatenate([collected, partner], axis=0),
        )
    own_cols = lax.dynamic_slice_in_dim(collected, col_index * col_block, col_block, 0)
    outer = (
        row_side.astype(jnp.float32)[:, None, :, None]
        * own_cols.astype(jnp.float32)[None, :, None, :]
    ).astype(jnp.bfloat16)
    outer = outer.reshape(pooled_rows * col_block, OPM * OPM)
    update = jnp.dot(outer, opm_weight, preferred_element_type=jnp.float32).reshape(pair_in.shape)
    pair_out = (pair_in.astype(jnp.float32) + update + pair_bias).astype(jnp.bfloat16)
    return (trunk_out, pair_out)


def solution(mesh):
    return jax.shard_map(
        per_device,
        mesh=mesh,
        in_specs=(
            P("col", "row"),
            P(None, "col", None),
            P("col"),
            P(),
            P(),
            P("row", "col", None),
            P(),
            P(),
        ),
        out_specs=(P("col", "row"), P("row", "col", None)),
        check_vma=False,
    )
```

```python
import jax
import jax.numpy as jnp
from jax import lax
from jax.sharding import PartitionSpec as P
from jax.experimental import pallas as pl
from jax.experimental.pallas import tpu as pltpu

TRUNK_CHANNELS = 1536
DILATION_STEP = 8
POOL = 16
OPM = 32

EPSILON = 1e-05


def with_halo(cells, sides, width):
    for axis, dim in sides:
        count = lax.axis_size(axis)
        ends = count - 1
        head = lax.slice_in_dim(cells, 0, width, axis=dim)
        tail = lax.slice_in_dim(cells, cells.shape[dim] - width, cells.shape[dim], axis=dim)
        cells = jnp.concatenate(
            [
                lax.ppermute(tail, axis, [(i, (i + 1) % count) for i in range(ends)]),
                cells,
                lax.ppermute(head, axis, [((i + 1) % count, i) for i in range(ends)]),
            ],
            axis=dim,
        )
    return cells


def partner_2(block, axis, bit):
    count = lax.axis_size(axis)
    route = []
    for low in range(count):
        high = low | 1 << bit
        if high != low and high < count:
            route += [(low, high), (high, low)]
    return lax.ppermute(block, axis, route)


def peer_of(index, step, count):
    if count & (count - 1) == 0:
        return index ^ step
    return (index + step) % count


def from_peer(block, axis, step):
    count = lax.axis_size(axis)
    if count & (count - 1) == 0:
        route = [(i, i ^ step) for i in range(count)]
    else:
        route = [((i + step) % count, i) for i in range(count)]
    return lax.ppermute(block, axis, route)


LANE = 128
SLAB = 256


def conv_kernel(n_src, kernel, local_channels, token_positions):
    border = (kernel // 2) * DILATION_STEP

    def body(ids_ref, gain_ref, bias_ref, proj_ref, *refs):
        core_hbm = refs[:n_src]
        edge_hbm = refs[n_src : 2 * n_src]
        w_hbm = refs[2 * n_src]
        (out_ref, side_ref, act_ref, w_buf, acc_ref, core_buf, edge_buf, pooled_buf, sems,
         in_sems) = refs[2 * n_src + 1 :]
        inputs = [
            pltpu.make_async_copy(core_hbm[s], core_buf.at[s], in_sems.at[s]) for s in range(n_src)
        ] + [
            pltpu.make_async_copy(edge_hbm[s], edge_buf.at[s], in_sems.at[n_src + s])
            for s in range(n_src)
        ]
        for copy in inputs:
            copy.start()
        copies = [
            pltpu.make_async_copy(w_hbm.at[tap], w_buf.at[tap], sems.at[tap])
            for tap in range(kernel)
        ]
        for copy in copies:
            copy.start()
        cores = [core_buf.at[s] for s in range(n_src)]
        edges = [edge_buf.at[s] for s in range(n_src)]
        chunks = list(range(0, token_positions, SLAB))
        core_totals = [None] * len(chunks)
        edge_total = None
        for s in range(n_src):
            inputs[s].wait()
            inputs[n_src + s].wait()
            for index, lo in enumerate(chunks):
                raw = cores[s][:, lo : lo + SLAB].astype(jnp.float32)
                part = jnp.sum(raw * raw, axis=0, keepdims=True)
                core_totals[index] = part if s == 0 else core_totals[index] + part
            raw = edges[s][...].astype(jnp.float32)
            part = jnp.sum(raw * raw, axis=0, keepdims=True)
            edge_total = part if s == 0 else edge_total + part
        core_scales = [lax.rsqrt(total / TRUNK_CHANNELS + EPSILON) for total in core_totals]
        edge_scale = lax.rsqrt(edge_total / TRUNK_CHANNELS + EPSILON)
        for s in range(n_src):
            row0 = pl.multiple_of(ids_ref[s] * local_channels, 8)
            gain = gain_ref[pl.ds(row0, local_channels), :]
            for lo, scl in zip(range(0, token_positions, SLAB), core_scales):
                raw = cores[s][:, lo : lo + SLAB].astype(jnp.float32)
                act_ref[pl.ds(row0, local_channels), LANE + lo : LANE + lo + SLAB] = jax.nn.gelu(
                    raw * gain * scl
                )
            edge = jax.nn.gelu(edges[s][...].astype(jnp.float32) * gain * edge_scale)
            act_ref[pl.ds(row0, local_channels), LANE - border : LANE] = edge[:, :border]
            act_ref[pl.ds(row0, local_channels), LANE + token_positions : LANE + token_positions + border] = edge[:, border:]
        centre = kernel // 2
        for tap in range(kernel):
            copies[tap].wait()
            start = LANE + (tap - centre) * DILATION_STEP
            for lo in range(0, token_positions, SLAB):
                rhs = act_ref[:, start + lo : start + lo + SLAB].astype(jnp.bfloat16)
                term = jnp.dot(w_buf[tap], rhs, preferred_element_type=jnp.float32)
                if tap == 0:
                    acc_ref[:, lo : lo + SLAB] = term
                else:
                    acc_ref[:, lo : lo + SLAB] += term
        pool_rows = lax.broadcasted_iota(jnp.int32, (SLAB, SLAB // POOL), 0) // POOL
        pool_cols = lax.broadcasted_iota(jnp.int32, (SLAB, SLAB // POOL), 1)
        pool = jnp.where(pool_rows == pool_cols, 1.0 / POOL, 0.0).astype(jnp.bfloat16)
        for lo in range(0, token_positions, SLAB):
            out = (
                cores[0][:, lo : lo + SLAB].astype(jnp.float32)
                + acc_ref[:, lo : lo + SLAB]
                + bias_ref[...]
            ).astype(jnp.bfloat16)
            out_ref[:, lo : lo + SLAB] = out
            pooled_buf[:, lo // POOL : (lo + SLAB) // POOL] = jnp.dot(
                out, pool, preferred_element_type=jnp.float32
            )
        pooled = pooled_buf[...].astype(jnp.bfloat16)
        side_ref[: proj_ref.shape[0], :] = jnp.dot(
            proj_ref[...], pooled, preferred_element_type=jnp.float32
        )
        pooled_f = pooled.astype(jnp.float32)
        side_ref[proj_ref.shape[0] :, :] = jnp.sum(pooled_f * pooled_f, axis=0, keepdims=True)

    return body


def fused_conv(ids, gains, bias, own_proj, cores, edges, weights):
    n_src = len(cores)
    kernel, local_channels, all_channels = weights.shape
    token_positions = cores[0].shape[1]
    width = token_positions + 2 * LANE
    sides = own_proj.shape[0]
    vmem = pl.BlockSpec(memory_space=pltpu.VMEM)
    anywhere = pl.BlockSpec(memory_space=pl.ANY)
    return pl.pallas_call(
        conv_kernel(n_src, kernel, local_channels, token_positions),
        out_shape=(
            jax.ShapeDtypeStruct((local_channels, token_positions), jnp.bfloat16),
            jax.ShapeDtypeStruct((sides + 1, token_positions // POOL), jnp.float32),
        ),
        in_specs=[pl.BlockSpec(memory_space=pltpu.SMEM), vmem, vmem, vmem]
        + [anywhere] * (2 * n_src + 1),
        out_specs=(vmem, vmem),
        scratch_shapes=[
            pltpu.VMEM((all_channels, width), jnp.float32),
            pltpu.VMEM((kernel, local_channels, all_channels), jnp.bfloat16),
            pltpu.VMEM((local_channels, token_positions), jnp.float32),
            pltpu.VMEM((n_src, local_channels, token_positions), jnp.bfloat16),
            pltpu.VMEM((n_src,) + edges[0].shape, jnp.bfloat16),
            pltpu.VMEM((local_channels, token_positions // POOL), jnp.float32),
            pltpu.SemaphoreType.DMA((kernel,)),
            pltpu.SemaphoreType.DMA((2 * n_src,)),
        ],
        compiler_params=pltpu.CompilerParams(vmem_limit_bytes=60 * 1024 * 1024),
    )(ids, gains, bias, own_proj, *cores, *edges, weights)


def per_device(
    trunk_in, conv_weight, conv_bias, norm_gain, pair_proj, pair_in, opm_weight, pair_bias
):
    local_channels = trunk_in.shape[0]
    token_positions = trunk_in.shape[1]
    kernel = conv_weight.shape[0]
    border_width = (kernel // 2) * DILATION_STEP
    n_col = lax.axis_size("col")
    row_index = lax.axis_index("row")
    col_index = lax.axis_index("col")

    n_row = lax.axis_size("row")
    from_left = lax.ppermute(
        trunk_in[:, token_positions - border_width :], "row", [(i, i + 1) for i in range(n_row - 1)]
    )
    from_right = lax.ppermute(
        trunk_in[:, :border_width], "row", [(i + 1, i) for i in range(n_row - 1)]
    )
    cores = [from_peer(trunk_in, "col", step) for step in range(1, n_col)]
    own_edges = jnp.concatenate([from_left, from_right], axis=1)
    edges = [from_peer(own_edges, "col", step) for step in range(1, n_col)]

    ids = jnp.stack([col_index] + [peer_of(col_index, step, n_col) for step in range(1, n_col)])
    ids = ids.astype(jnp.int32)
    own_proj = lax.dynamic_slice_in_dim(pair_proj, col_index * local_channels, local_channels, 1)
    trunk_out, packed = fused_conv(
        ids,
        norm_gain[:, None],
        conv_bias[:, None],
        own_proj,
        [trunk_in] + cores,
        [own_edges] + edges,
        conv_weight,
    )
    everyone = lax.all_to_all(
        jnp.broadcast_to(packed[None], (n_col,) + packed.shape), "col", 0, 0, tiled=False
    )
    total = jnp.sum(everyone, axis=0).T
    side_width = total.shape[1] - 1
    projected = total[:, :side_width]
    sums = total[:, side_width]
    sides = (projected * lax.rsqrt(sums / TRUNK_CHANNELS + EPSILON)[:, None]).astype(jnp.bfloat16)
    row_side = sides[:, :OPM]
    collected = sides[:, OPM:]
    col_block = pair_in.shape[1]
    pooled_rows = row_side.shape[0]
    per_window = col_block * n_col // pooled_rows
    in_window = row_index % per_window
    for bit_num in range(per_window.bit_length() - 1):
        partner = partner_2(collected, "row", bit_num)
        upper_half = in_window // 2**bit_num % 2 == 1
        collected = jnp.where(
            upper_half,
            jnp.concatenate([partner, collected], axis=0),
            jnp.concatenate([collected, partner], axis=0),
        )
    own_cols = lax.dynamic_slice_in_dim(collected, col_index * col_block, col_block, 0)
    outer = (
        row_side.astype(jnp.float32)[:, None, :, None]
        * own_cols.astype(jnp.float32)[None, :, None, :]
    ).astype(jnp.bfloat16)
    outer = outer.reshape(pooled_rows * col_block, OPM * OPM)
    update = jnp.dot(outer, opm_weight, preferred_element_type=jnp.float32).reshape(pair_in.shape)
    pair_out = (pair_in.astype(jnp.float32) + update + pair_bias).astype(jnp.bfloat16)
    return (trunk_out, pair_out)


def solution(mesh):
    return jax.shard_map(
        per_device,
        mesh=mesh,
        in_specs=(
            P("col", "row"),
            P(None, "col", None),
            P("col"),
            P(),
            P(),
            P("row", "col", None),
            P(),
            P(),
        ),
        out_specs=(P("col", "row"), P("row", "col", None)),
        check_vma=False,
    )
```

```python
import jax
import jax.numpy as jnp
from jax import lax
from jax.sharding import PartitionSpec as P
from jax.experimental import pallas as pl
from jax.experimental.pallas import tpu as pltpu

TRUNK_CHANNELS = 1536
DILATION_STEP = 8
POOL = 16
OPM = 32

EPSILON = 1e-05


def with_halo(cells, sides, width):
    for axis, dim in sides:
        count = lax.axis_size(axis)
        ends = count - 1
        head = lax.slice_in_dim(cells, 0, width, axis=dim)
        tail = lax.slice_in_dim(cells, cells.shape[dim] - width, cells.shape[dim], axis=dim)
        cells = jnp.concatenate(
            [
                lax.ppermute(tail, axis, [(i, (i + 1) % count) for i in range(ends)]),
                cells,
                lax.ppermute(head, axis, [((i + 1) % count, i) for i in range(ends)]),
            ],
            axis=dim,
        )
    return cells


def partner_2(block, axis, bit):
    count = lax.axis_size(axis)
    route = []
    for low in range(count):
        high = low | 1 << bit
        if high != low and high < count:
            route += [(low, high), (high, low)]
    return lax.ppermute(block, axis, route)


def peer_of(index, step, count):
    if count & (count - 1) == 0:
        return index ^ step
    return (index + step) % count


def from_peer(block, axis, step):
    count = lax.axis_size(axis)
    if count & (count - 1) == 0:
        route = [(i, i ^ step) for i in range(count)]
    else:
        route = [((i + step) % count, i) for i in range(count)]
    return lax.ppermute(block, axis, route)


LANE = 128
SLAB = 256


def conv_kernel(n_src, kernel, local_channels, token_positions):
    border = (kernel // 2) * DILATION_STEP

    def body(ids_ref, gain_ref, bias_ref, proj_ref, *refs):
        cores = refs[:n_src]
        edges = refs[n_src : 2 * n_src]
        w_hbm = refs[2 * n_src]
        out_ref, side_ref, act_ref, w_buf, acc_ref, pooled_buf, sems = refs[2 * n_src + 1 :]
        copies = [
            pltpu.make_async_copy(w_hbm.at[tap], w_buf.at[tap], sems.at[tap])
            for tap in range(kernel)
        ]
        for copy in copies:
            copy.start()
        core_scales = []
        for lo in range(0, token_positions, SLAB):
            total = None
            for s in range(n_src):
                raw = cores[s][:, lo : lo + SLAB].astype(jnp.float32)
                part = jnp.sum(raw * raw, axis=0, keepdims=True)
                total = part if total is None else total + part
            core_scales.append(lax.rsqrt(total / TRUNK_CHANNELS + EPSILON))
        total = None
        for s in range(n_src):
            raw = edges[s][...].astype(jnp.float32)
            part = jnp.sum(raw * raw, axis=0, keepdims=True)
            total = part if total is None else total + part
        edge_scale = lax.rsqrt(total / TRUNK_CHANNELS + EPSILON)
        for s in range(n_src):
            row0 = pl.multiple_of(ids_ref[s] * local_channels, 8)
            gain = gain_ref[pl.ds(row0, local_channels), :]
            for lo, scl in zip(range(0, token_positions, SLAB), core_scales):
                raw = cores[s][:, lo : lo + SLAB].astype(jnp.float32)
                act_ref[pl.ds(row0, local_channels), LANE + lo : LANE + lo + SLAB] = jax.nn.gelu(
                    raw * gain * scl
                )
            edge = jax.nn.gelu(edges[s][...].astype(jnp.float32) * gain * edge_scale)
            act_ref[pl.ds(row0, local_channels), LANE - border : LANE] = edge[:, :border]
            act_ref[pl.ds(row0, local_channels), LANE + token_positions : LANE + token_positions + border] = edge[:, border:]
        centre = kernel // 2
        for tap in range(kernel):
            copies[tap].wait()
            start = LANE + (tap - centre) * DILATION_STEP
            for lo in range(0, token_positions, SLAB):
                rhs = act_ref[:, start + lo : start + lo + SLAB].astype(jnp.bfloat16)
                term = jnp.dot(w_buf[tap], rhs, preferred_element_type=jnp.float32)
                if tap == 0:
                    acc_ref[:, lo : lo + SLAB] = term
                else:
                    acc_ref[:, lo : lo + SLAB] += term
        pool_rows = lax.broadcasted_iota(jnp.int32, (SLAB, SLAB // POOL), 0) // POOL
        pool_cols = lax.broadcasted_iota(jnp.int32, (SLAB, SLAB // POOL), 1)
        pool = jnp.where(pool_rows == pool_cols, 1.0 / POOL, 0.0).astype(jnp.bfloat16)
        for lo in range(0, token_positions, SLAB):
            out = (
                cores[0][:, lo : lo + SLAB].astype(jnp.float32)
                + acc_ref[:, lo : lo + SLAB]
                + bias_ref[...]
            ).astype(jnp.bfloat16)
            out_ref[:, lo : lo + SLAB] = out
            pooled_buf[:, lo // POOL : (lo + SLAB) // POOL] = jnp.dot(
                out, pool, preferred_element_type=jnp.float32
            )
        pooled = pooled_buf[...].astype(jnp.bfloat16)
        side_ref[: proj_ref.shape[0], :] = jnp.dot(
            proj_ref[...], pooled, preferred_element_type=jnp.float32
        )
        pooled_f = pooled.astype(jnp.float32)
        side_ref[proj_ref.shape[0] :, :] = jnp.sum(pooled_f * pooled_f, axis=0, keepdims=True)

    return body


def fused_conv(ids, gains, bias, own_proj, cores, edges, weights):
    n_src = len(cores)
    kernel, local_channels, all_channels = weights.shape
    token_positions = cores[0].shape[1]
    width = token_positions + 2 * LANE
    vmem = pl.BlockSpec(memory_space=pltpu.VMEM)
    return pl.pallas_call(
        conv_kernel(n_src, kernel, local_channels, token_positions),
        out_shape=(
            jax.ShapeDtypeStruct((local_channels, token_positions), jnp.bfloat16),
            jax.ShapeDtypeStruct((own_proj.shape[0] + 1, token_positions // POOL), jnp.float32),
        ),
        in_specs=[pl.BlockSpec(memory_space=pltpu.SMEM), vmem, vmem, vmem]
        + [vmem] * (2 * n_src)
        + [pl.BlockSpec(memory_space=pl.ANY)],
        out_specs=(vmem, vmem),
        scratch_shapes=[
            pltpu.VMEM((all_channels, width), jnp.float32),
            pltpu.VMEM((kernel, local_channels, all_channels), jnp.bfloat16),
            pltpu.VMEM((local_channels, token_positions), jnp.float32),
            pltpu.VMEM((local_channels, token_positions // POOL), jnp.float32),
            pltpu.SemaphoreType.DMA((kernel,)),
        ],
        compiler_params=pltpu.CompilerParams(vmem_limit_bytes=60 * 1024 * 1024),
    )(ids, gains, bias, own_proj, *cores, *edges, weights)


def per_device(
    trunk_in, conv_weight, conv_bias, norm_gain, pair_proj, pair_in, opm_weight, pair_bias
):
    local_channels = trunk_in.shape[0]
    token_positions = trunk_in.shape[1]
    kernel = conv_weight.shape[0]
    border_width = (kernel // 2) * DILATION_STEP
    n_col = lax.axis_size("col")
    row_index = lax.axis_index("row")
    col_index = lax.axis_index("col")

    n_row = lax.axis_size("row")
    from_left = lax.ppermute(
        trunk_in[:, token_positions - border_width :], "row", [(i, i + 1) for i in range(n_row - 1)]
    )
    from_right = lax.ppermute(
        trunk_in[:, :border_width], "row", [(i + 1, i) for i in range(n_row - 1)]
    )
    cores = [from_peer(trunk_in, "col", step) for step in range(1, n_col)]
    own_edges = jnp.concatenate([from_left, from_right], axis=1)
    edges = [from_peer(own_edges, "col", step) for step in range(1, n_col)]

    ids = jnp.stack([col_index] + [peer_of(col_index, step, n_col) for step in range(1, n_col)])
    ids = ids.astype(jnp.int32)
    own_proj = lax.dynamic_slice_in_dim(pair_proj, col_index * local_channels, local_channels, 1)
    trunk_out, packed = fused_conv(
        ids,
        norm_gain[:, None],
        conv_bias[:, None],
        own_proj,
        [trunk_in] + cores,
        [own_edges] + edges,
        conv_weight,
    )
    total = packed
    for step in range(1, n_col):
        total = total + from_peer(packed, "col", step)
    total = total.T
    side_width = total.shape[1] - 1
    projected = total[:, :side_width]
    sums = total[:, side_width]
    sides = (projected * lax.rsqrt(sums / TRUNK_CHANNELS + EPSILON)[:, None]).astype(jnp.bfloat16)
    row_side = sides[:, :OPM]
    collected = sides[:, OPM:]
    col_block = pair_in.shape[1]
    pooled_rows = row_side.shape[0]
    per_window = col_block * n_col // pooled_rows
    in_window = row_index % per_window
    for bit_num in range(per_window.bit_length() - 1):
        partner = partner_2(collected, "row", bit_num)
        upper_half = in_window // 2**bit_num % 2 == 1
        collected = jnp.where(
            upper_half,
            jnp.concatenate([partner, collected], axis=0),
            jnp.concatenate([collected, partner], axis=0),
        )
    own_cols = lax.dynamic_slice_in_dim(collected, col_index * col_block, col_block, 0)
    outer = (
        row_side.astype(jnp.float32)[:, None, :, None]
        * own_cols.astype(jnp.float32)[None, :, None, :]
    ).astype(jnp.bfloat16)
    outer = outer.reshape(pooled_rows * col_block, OPM * OPM)
    update = jnp.dot(outer, opm_weight, preferred_element_type=jnp.float32).reshape(pair_in.shape)
    pair_out = (pair_in.astype(jnp.float32) + update + pair_bias).astype(jnp.bfloat16)
    return (trunk_out, pair_out)


def solution(mesh):
    return jax.shard_map(
        per_device,
        mesh=mesh,
        in_specs=(
            P("col", "row"),
            P(None, "col", None),
            P("col"),
            P(),
            P(),
            P("row", "col", None),
            P(),
            P(),
        ),
        out_specs=(P("col", "row"), P("row", "col", None)),
        check_vma=False,
    )
```

```python
import jax
import jax.numpy as jnp
from jax import lax
from jax.sharding import PartitionSpec as P
from jax.experimental import pallas as pl
from jax.experimental.pallas import tpu as pltpu

TRUNK_CHANNELS = 1536
DILATION_STEP = 8
POOL = 16
OPM = 32

EPSILON = 1e-05


def with_halo(cells, sides, width):
    for axis, dim in sides:
        count = lax.axis_size(axis)
        ends = count - 1
        head = lax.slice_in_dim(cells, 0, width, axis=dim)
        tail = lax.slice_in_dim(cells, cells.shape[dim] - width, cells.shape[dim], axis=dim)
        cells = jnp.concatenate(
            [
                lax.ppermute(tail, axis, [(i, (i + 1) % count) for i in range(ends)]),
                cells,
                lax.ppermute(head, axis, [((i + 1) % count, i) for i in range(ends)]),
            ],
            axis=dim,
        )
    return cells


def partner_2(block, axis, bit):
    count = lax.axis_size(axis)
    route = []
    for low in range(count):
        high = low | 1 << bit
        if high != low and high < count:
            route += [(low, high), (high, low)]
    return lax.ppermute(block, axis, route)


def peer_of(index, step, count):
    if count & (count - 1) == 0:
        return index ^ step
    return (index + step) % count


def from_peer(block, axis, step):
    count = lax.axis_size(axis)
    if count & (count - 1) == 0:
        route = [(i, i ^ step) for i in range(count)]
    else:
        route = [((i + step) % count, i) for i in range(count)]
    return lax.ppermute(block, axis, route)


LANE = 128
SLAB = 256


def conv_kernel(n_src, kernel, local_channels, token_positions):
    border = (kernel // 2) * DILATION_STEP

    def body(ids_ref, gain_ref, bias_ref, proj_ref, *refs):
        cores = refs[:n_src]
        edges = refs[n_src : 2 * n_src]
        w_hbm = refs[2 * n_src]
        out_ref, side_ref, act_ref, w_buf, acc_ref, pooled_buf, sems = refs[2 * n_src + 1 :]
        copies = [
            pltpu.make_async_copy(w_hbm.at[tap], w_buf.at[tap], sems.at[tap])
            for tap in range(kernel)
        ]
        for copy in copies:
            copy.start()
        core_scales = []
        for lo in range(0, token_positions, SLAB):
            total = None
            for s in range(n_src):
                raw = cores[s][:, lo : lo + SLAB].astype(jnp.float32)
                part = jnp.sum(raw * raw, axis=0, keepdims=True)
                total = part if total is None else total + part
            core_scales.append(lax.rsqrt(total / TRUNK_CHANNELS + EPSILON))
        total = None
        for s in range(n_src):
            raw = edges[s][...].astype(jnp.float32)
            part = jnp.sum(raw * raw, axis=0, keepdims=True)
            total = part if total is None else total + part
        edge_scale = lax.rsqrt(total / TRUNK_CHANNELS + EPSILON)
        for s in range(n_src):
            row0 = pl.multiple_of(ids_ref[s] * local_channels, 8)
            gain = gain_ref[pl.ds(row0, local_channels), :]
            for lo, scl in zip(range(0, token_positions, SLAB), core_scales):
                raw = cores[s][:, lo : lo + SLAB].astype(jnp.float32)
                act_ref[pl.ds(row0, local_channels), LANE + lo : LANE + lo + SLAB] = jax.nn.gelu(
                    raw * gain * scl
                ).astype(act_ref.dtype)
            edge = jax.nn.gelu(edges[s][...].astype(jnp.float32) * gain * edge_scale).astype(
                act_ref.dtype
            )
            act_ref[pl.ds(row0, local_channels), LANE - border : LANE] = edge[:, :border]
            act_ref[pl.ds(row0, local_channels), LANE + token_positions : LANE + token_positions + border] = edge[:, border:]
        centre = kernel // 2
        for tap in range(kernel):
            copies[tap].wait()
            start = LANE + (tap - centre) * DILATION_STEP
            for lo in range(0, token_positions, SLAB):
                rhs = act_ref[:, start + lo : start + lo + SLAB]
                term = jnp.dot(w_buf[tap], rhs, preferred_element_type=jnp.float32)
                if tap == 0:
                    acc_ref[:, lo : lo + SLAB] = term
                else:
                    acc_ref[:, lo : lo + SLAB] += term
        pool_rows = lax.broadcasted_iota(jnp.int32, (SLAB, SLAB // POOL), 0) // POOL
        pool_cols = lax.broadcasted_iota(jnp.int32, (SLAB, SLAB // POOL), 1)
        pool = jnp.where(pool_rows == pool_cols, 1.0 / POOL, 0.0).astype(jnp.bfloat16)
        for lo in range(0, token_positions, SLAB):
            out = (
                cores[0][:, lo : lo + SLAB].astype(jnp.float32)
                + acc_ref[:, lo : lo + SLAB]
                + bias_ref[...]
            ).astype(jnp.bfloat16)
            out_ref[:, lo : lo + SLAB] = out
            pooled_buf[:, lo // POOL : (lo + SLAB) // POOL] = jnp.dot(
                out, pool, preferred_element_type=jnp.float32
            )
        pooled = pooled_buf[...].astype(jnp.bfloat16)
        side_ref[: proj_ref.shape[0], :] = jnp.dot(
            proj_ref[...], pooled, preferred_element_type=jnp.float32
        )
        pooled_f = pooled.astype(jnp.float32)
        side_ref[proj_ref.shape[0] :, :] = jnp.sum(pooled_f * pooled_f, axis=0, keepdims=True)

    return body


def fused_conv(ids, gains, bias, own_proj, cores, edges, weights):
    n_src = len(cores)
    kernel, local_channels, all_channels = weights.shape
    token_positions = cores[0].shape[1]
    width = token_positions + 2 * LANE
    vmem = pl.BlockSpec(memory_space=pltpu.VMEM)
    return pl.pallas_call(
        conv_kernel(n_src, kernel, local_channels, token_positions),
        out_shape=(
            jax.ShapeDtypeStruct((local_channels, token_positions), jnp.bfloat16),
            jax.ShapeDtypeStruct((own_proj.shape[0] + 1, token_positions // POOL), jnp.float32),
        ),
        in_specs=[pl.BlockSpec(memory_space=pltpu.SMEM), vmem, vmem, vmem]
        + [vmem] * (2 * n_src)
        + [pl.BlockSpec(memory_space=pl.ANY)],
        out_specs=(vmem, vmem),
        scratch_shapes=[
            pltpu.VMEM((all_channels, width), jnp.bfloat16),
            pltpu.VMEM((kernel, local_channels, all_channels), jnp.bfloat16),
            pltpu.VMEM((local_channels, token_positions), jnp.float32),
            pltpu.VMEM((local_channels, token_positions // POOL), jnp.float32),
            pltpu.SemaphoreType.DMA((kernel,)),
        ],
        compiler_params=pltpu.CompilerParams(vmem_limit_bytes=60 * 1024 * 1024),
    )(ids, gains, bias, own_proj, *cores, *edges, weights)


def per_device(
    trunk_in, conv_weight, conv_bias, norm_gain, pair_proj, pair_in, opm_weight, pair_bias
):
    local_channels = trunk_in.shape[0]
    token_positions = trunk_in.shape[1]
    kernel = conv_weight.shape[0]
    border_width = (kernel // 2) * DILATION_STEP
    n_col = lax.axis_size("col")
    row_index = lax.axis_index("row")
    col_index = lax.axis_index("col")

    n_row = lax.axis_size("row")
    from_left = lax.ppermute(
        trunk_in[:, token_positions - border_width :], "row", [(i, i + 1) for i in range(n_row - 1)]
    )
    from_right = lax.ppermute(
        trunk_in[:, :border_width], "row", [(i + 1, i) for i in range(n_row - 1)]
    )
    cores = [from_peer(trunk_in, "col", step) for step in range(1, n_col)]
    own_edges = jnp.concatenate([from_left, from_right], axis=1)
    edges = [from_peer(own_edges, "col", step) for step in range(1, n_col)]

    ids = jnp.stack([col_index] + [peer_of(col_index, step, n_col) for step in range(1, n_col)])
    ids = ids.astype(jnp.int32)
    own_proj = lax.dynamic_slice_in_dim(pair_proj, col_index * local_channels, local_channels, 1)
    trunk_out, packed = fused_conv(
        ids,
        norm_gain[:, None],
        conv_bias[:, None],
        own_proj,
        [trunk_in] + cores,
        [own_edges] + edges,
        conv_weight,
    )
    total = packed
    for step in range(1, n_col):
        total = total + from_peer(packed, "col", step)
    total = total.T
    side_width = total.shape[1] - 1
    projected = total[:, :side_width]
    sums = total[:, side_width]
    sides = (projected * lax.rsqrt(sums / TRUNK_CHANNELS + EPSILON)[:, None]).astype(jnp.bfloat16)
    row_side = sides[:, :OPM]
    collected = sides[:, OPM:]
    col_block = pair_in.shape[1]
    pooled_rows = row_side.shape[0]
    per_window = col_block * n_col // pooled_rows
    in_window = row_index % per_window
    for bit_num in range(per_window.bit_length() - 1):
        partner = partner_2(collected, "row", bit_num)
        upper_half = in_window // 2**bit_num % 2 == 1
        collected = jnp.where(
            upper_half,
            jnp.concatenate([partner, collected], axis=0),
            jnp.concatenate([collected, partner], axis=0),
        )
    own_cols = lax.dynamic_slice_in_dim(collected, col_index * col_block, col_block, 0)
    outer = (
        row_side.astype(jnp.float32)[:, None, :, None]
        * own_cols.astype(jnp.float32)[None, :, None, :]
    ).astype(jnp.bfloat16)
    outer = outer.reshape(pooled_rows * col_block, OPM * OPM)
    update = jnp.dot(outer, opm_weight, preferred_element_type=jnp.float32).reshape(pair_in.shape)
    pair_out = (pair_in.astype(jnp.float32) + update + pair_bias).astype(jnp.bfloat16)
    return (trunk_out, pair_out)


def solution(mesh):
    return jax.shard_map(
        per_device,
        mesh=mesh,
        in_specs=(
            P("col", "row"),
            P(None, "col", None),
            P("col"),
            P(),
            P(),
            P("row", "col", None),
            P(),
            P(),
        ),
        out_specs=(P("col", "row"), P("row", "col", None)),
        check_vma=False,
    )
```

```python
import jax
import jax.numpy as jnp
from jax import lax
from jax.sharding import PartitionSpec as P
from jax.experimental import pallas as pl
from jax.experimental.pallas import tpu as pltpu

TRUNK_CHANNELS = 1536
DILATION_STEP = 8
POOL = 16
OPM = 32

EPSILON = 1e-05


def with_halo(cells, sides, width):
    for axis, dim in sides:
        count = lax.axis_size(axis)
        ends = count - 1
        head = lax.slice_in_dim(cells, 0, width, axis=dim)
        tail = lax.slice_in_dim(cells, cells.shape[dim] - width, cells.shape[dim], axis=dim)
        cells = jnp.concatenate(
            [
                lax.ppermute(tail, axis, [(i, (i + 1) % count) for i in range(ends)]),
                cells,
                lax.ppermute(head, axis, [((i + 1) % count, i) for i in range(ends)]),
            ],
            axis=dim,
        )
    return cells


def partner_2(block, axis, bit):
    count = lax.axis_size(axis)
    route = []
    for low in range(count):
        high = low | 1 << bit
        if high != low and high < count:
            route += [(low, high), (high, low)]
    return lax.ppermute(block, axis, route)


def peer_of(index, step, count):
    if count & (count - 1) == 0:
        return index ^ step
    return (index + step) % count


def from_peer(block, axis, step):
    count = lax.axis_size(axis)
    if count & (count - 1) == 0:
        route = [(i, i ^ step) for i in range(count)]
    else:
        route = [((i + step) % count, i) for i in range(count)]
    return lax.ppermute(block, axis, route)


LANE = 128
SLAB = 256


def conv_kernel(n_src, kernel, local_channels, token_positions):
    border = (kernel // 2) * DILATION_STEP
    static_rows = local_channels % LANE == 0 and n_src % 2 == 0
    groups = [(s, s + 1) for s in range(0, n_src, 2)] if static_rows else [tuple(range(n_src))]

    def body(ids_ref, gain_ref, bias_ref, proj_ref, *refs):
        cores = refs[:n_src]
        edges = refs[n_src : 2 * n_src]
        w_hbm = refs[2 * n_src]
        out_ref, side_ref, act_ref, w_buf, acc_ref, pooled_buf, sems = refs[2 * n_src + 1 :]
        if static_rows:
            copies = [
                [
                    pltpu.make_async_copy(
                        w_hbm.at[tap, :, pl.ds(pl.multiple_of(ids_ref[s] * local_channels, LANE), local_channels)],
                        w_buf.at[tap, :, pl.ds(s * local_channels, local_channels)],
                        sems.at[tap * n_src + s],
                    )
                    for s in range(n_src)
                ]
                for tap in range(kernel)
            ]
        else:
            copies = [
                [pltpu.make_async_copy(w_hbm.at[tap], w_buf.at[tap], sems.at[tap * n_src])]
                for tap in range(kernel)
            ]
        for tap_copies in copies:
            for copy in tap_copies:
                copy.start()
        core_scales = []
        for lo in range(0, token_positions, SLAB):
            total = None
            for s in range(n_src):
                raw = cores[s][:, lo : lo + SLAB].astype(jnp.float32)
                part = jnp.sum(raw * raw, axis=0, keepdims=True)
                total = part if total is None else total + part
            core_scales.append(lax.rsqrt(total / TRUNK_CHANNELS + EPSILON))
        total = None
        for s in range(n_src):
            raw = edges[s][...].astype(jnp.float32)
            part = jnp.sum(raw * raw, axis=0, keepdims=True)
            total = part if total is None else total + part
        edge_scale = lax.rsqrt(total / TRUNK_CHANNELS + EPSILON)
        centre = kernel // 2
        for number, group in enumerate(groups):
            for s in group:
                if static_rows:
                    row0 = s * local_channels
                    gain = gain_ref[pl.ds(pl.multiple_of(ids_ref[s] * local_channels, 8), local_channels), :]
                else:
                    row0 = pl.multiple_of(ids_ref[s] * local_channels, 8)
                    gain = gain_ref[pl.ds(row0, local_channels), :]
                rows = pl.ds(row0, local_channels)
                for lo, scl in zip(range(0, token_positions, SLAB), core_scales):
                    raw = cores[s][:, lo : lo + SLAB].astype(jnp.float32)
                    act_ref[rows, LANE + lo : LANE + lo + SLAB] = jax.nn.gelu(
                        raw * gain * scl
                    ).astype(act_ref.dtype)
                edge = jax.nn.gelu(edges[s][...].astype(jnp.float32) * gain * edge_scale).astype(
                    act_ref.dtype
                )
                act_ref[rows, LANE - border : LANE] = edge[:, :border]
                act_ref[rows, LANE + token_positions : LANE + token_positions + border] = edge[:, border:]
            if static_rows:
                k_rows = slice(group[0] * local_channels, (group[-1] + 1) * local_channels)
            else:
                k_rows = slice(0, n_src * local_channels)
            for tap in range(kernel):
                if static_rows:
                    for s in group:
                        copies[tap][s].wait()
                elif number == 0:
                    copies[tap][0].wait()
                start = LANE + (tap - centre) * DILATION_STEP
                for lo in range(0, token_positions, SLAB):
                    rhs = act_ref[k_rows, start + lo : start + lo + SLAB]
                    term = jnp.dot(
                        w_buf[tap, :, k_rows], rhs, preferred_element_type=jnp.float32
                    )
                    if tap == 0 and number == 0:
                        acc_ref[:, lo : lo + SLAB] = term
                    else:
                        acc_ref[:, lo : lo + SLAB] += term
        pool_rows = lax.broadcasted_iota(jnp.int32, (SLAB, SLAB // POOL), 0) // POOL
        pool_cols = lax.broadcasted_iota(jnp.int32, (SLAB, SLAB // POOL), 1)
        pool = jnp.where(pool_rows == pool_cols, 1.0 / POOL, 0.0).astype(jnp.bfloat16)
        for lo in range(0, token_positions, SLAB):
            out = (
                cores[0][:, lo : lo + SLAB].astype(jnp.float32)
                + acc_ref[:, lo : lo + SLAB]
                + bias_ref[...]
            ).astype(jnp.bfloat16)
            out_ref[:, lo : lo + SLAB] = out
            pooled_buf[:, lo // POOL : (lo + SLAB) // POOL] = jnp.dot(
                out, pool, preferred_element_type=jnp.float32
            )
        pooled = pooled_buf[...].astype(jnp.bfloat16)
        side_ref[: proj_ref.shape[0], :] = jnp.dot(
            proj_ref[...], pooled, preferred_element_type=jnp.float32
        )
        pooled_f = pooled.astype(jnp.float32)
        side_ref[proj_ref.shape[0] :, :] = jnp.sum(pooled_f * pooled_f, axis=0, keepdims=True)

    return body


def fused_conv(ids, gains, bias, own_proj, cores, edges, weights):
    n_src = len(cores)
    kernel, local_channels, all_channels = weights.shape
    token_positions = cores[0].shape[1]
    width = token_positions + 2 * LANE
    vmem = pl.BlockSpec(memory_space=pltpu.VMEM)
    return pl.pallas_call(
        conv_kernel(n_src, kernel, local_channels, token_positions),
        out_shape=(
            jax.ShapeDtypeStruct((local_channels, token_positions), jnp.bfloat16),
            jax.ShapeDtypeStruct((own_proj.shape[0] + 1, token_positions // POOL), jnp.float32),
        ),
        in_specs=[pl.BlockSpec(memory_space=pltpu.SMEM), vmem, vmem, vmem]
        + [vmem] * (2 * n_src)
        + [pl.BlockSpec(memory_space=pl.ANY)],
        out_specs=(vmem, vmem),
        scratch_shapes=[
            pltpu.VMEM((all_channels, width), jnp.bfloat16),
            pltpu.VMEM((kernel, local_channels, all_channels), jnp.bfloat16),
            pltpu.VMEM((local_channels, token_positions), jnp.float32),
            pltpu.VMEM((local_channels, token_positions // POOL), jnp.float32),
            pltpu.SemaphoreType.DMA((kernel * n_src,)),
        ],
        compiler_params=pltpu.CompilerParams(vmem_limit_bytes=60 * 1024 * 1024),
    )(ids, gains, bias, own_proj, *cores, *edges, weights)


def per_device(
    trunk_in, conv_weight, conv_bias, norm_gain, pair_proj, pair_in, opm_weight, pair_bias
):
    local_channels = trunk_in.shape[0]
    token_positions = trunk_in.shape[1]
    kernel = conv_weight.shape[0]
    border_width = (kernel // 2) * DILATION_STEP
    n_col = lax.axis_size("col")
    row_index = lax.axis_index("row")
    col_index = lax.axis_index("col")

    n_row = lax.axis_size("row")
    from_left = lax.ppermute(
        trunk_in[:, token_positions - border_width :], "row", [(i, i + 1) for i in range(n_row - 1)]
    )
    from_right = lax.ppermute(
        trunk_in[:, :border_width], "row", [(i + 1, i) for i in range(n_row - 1)]
    )
    cores = [from_peer(trunk_in, "col", step) for step in range(1, n_col)]
    own_edges = jnp.concatenate([from_left, from_right], axis=1)
    edges = [from_peer(own_edges, "col", step) for step in range(1, n_col)]

    ids = jnp.stack([col_index] + [peer_of(col_index, step, n_col) for step in range(1, n_col)])
    ids = ids.astype(jnp.int32)
    own_proj = lax.dynamic_slice_in_dim(pair_proj, col_index * local_channels, local_channels, 1)
    trunk_out, packed = fused_conv(
        ids,
        norm_gain[:, None],
        conv_bias[:, None],
        own_proj,
        [trunk_in] + cores,
        [own_edges] + edges,
        conv_weight,
    )
    total = packed
    for step in range(1, n_col):
        total = total + from_peer(packed, "col", step)
    total = total.T
    side_width = total.shape[1] - 1
    projected = total[:, :side_width]
    sums = total[:, side_width]
    sides = (projected * lax.rsqrt(sums / TRUNK_CHANNELS + EPSILON)[:, None]).astype(jnp.bfloat16)
    row_side = sides[:, :OPM]
    collected = sides[:, OPM:]
    col_block = pair_in.shape[1]
    pooled_rows = row_side.shape[0]
    per_window = col_block * n_col // pooled_rows
    in_window = row_index % per_window
    for bit_num in range(per_window.bit_length() - 1):
        partner = partner_2(collected, "row", bit_num)
        upper_half = in_window // 2**bit_num % 2 == 1
        collected = jnp.where(
            upper_half,
            jnp.concatenate([partner, collected], axis=0),
            jnp.concatenate([collected, partner], axis=0),
        )
    own_cols = lax.dynamic_slice_in_dim(collected, col_index * col_block, col_block, 0)
    outer = (
        row_side.astype(jnp.float32)[:, None, :, None]
        * own_cols.astype(jnp.float32)[None, :, None, :]
    ).astype(jnp.bfloat16)
    outer = outer.reshape(pooled_rows * col_block, OPM * OPM)
    update = jnp.dot(outer, opm_weight, preferred_element_type=jnp.float32).reshape(pair_in.shape)
    pair_out = (pair_in.astype(jnp.float32) + update + pair_bias).astype(jnp.bfloat16)
    return (trunk_out, pair_out)


def solution(mesh):
    return jax.shard_map(
        per_device,
        mesh=mesh,
        in_specs=(
            P("col", "row"),
            P(None, "col", None),
            P("col"),
            P(),
            P(),
            P("row", "col", None),
            P(),
            P(),
        ),
        out_specs=(P("col", "row"), P("row", "col", None)),
        check_vma=False,
    )
```

```python
import jax
import jax.numpy as jnp
from jax import lax
from jax.sharding import PartitionSpec as P
from jax.experimental import pallas as pl
from jax.experimental.pallas import tpu as pltpu

TRUNK_CHANNELS = 1536
DILATION_STEP = 8
POOL = 16
OPM = 32

EPSILON = 1e-05


def with_halo(cells, sides, width):
    for axis, dim in sides:
        count = lax.axis_size(axis)
        ends = count - 1
        head = lax.slice_in_dim(cells, 0, width, axis=dim)
        tail = lax.slice_in_dim(cells, cells.shape[dim] - width, cells.shape[dim], axis=dim)
        cells = jnp.concatenate(
            [
                lax.ppermute(tail, axis, [(i, (i + 1) % count) for i in range(ends)]),
                cells,
                lax.ppermute(head, axis, [((i + 1) % count, i) for i in range(ends)]),
            ],
            axis=dim,
        )
    return cells


def partner_2(block, axis, bit):
    count = lax.axis_size(axis)
    route = []
    for low in range(count):
        high = low | 1 << bit
        if high != low and high < count:
            route += [(low, high), (high, low)]
    return lax.ppermute(block, axis, route)


def peer_of(index, step, count):
    if count & (count - 1) == 0:
        return index ^ step
    return (index + step) % count


def from_peer(block, axis, step):
    count = lax.axis_size(axis)
    if count & (count - 1) == 0:
        route = [(i, i ^ step) for i in range(count)]
    else:
        route = [((i + step) % count, i) for i in range(count)]
    return lax.ppermute(block, axis, route)


LANE = 128
SLAB = 256
MM_SLAB = 512


def conv_kernel(n_src, kernel, local_channels, token_positions):
    border = (kernel // 2) * DILATION_STEP

    def body(ids_ref, gain_ref, bias_ref, proj_ref, *refs):
        cores = refs[:n_src]
        edges = refs[n_src : 2 * n_src]
        w_hbm = refs[2 * n_src]
        out_ref, side_ref, act_ref, w_buf, acc_ref, pooled_buf, sems = refs[2 * n_src + 1 :]
        copies = [
            pltpu.make_async_copy(w_hbm.at[tap], w_buf.at[tap], sems.at[tap])
            for tap in range(kernel)
        ]
        for copy in copies:
            copy.start()
        core_scales = []
        for lo in range(0, token_positions, SLAB):
            total = None
            for s in range(n_src):
                raw = cores[s][:, lo : lo + SLAB].astype(jnp.float32)
                part = jnp.sum(raw * raw, axis=0, keepdims=True)
                total = part if total is None else total + part
            core_scales.append(lax.rsqrt(total / TRUNK_CHANNELS + EPSILON))
        total = None
        for s in range(n_src):
            raw = edges[s][...].astype(jnp.float32)
            part = jnp.sum(raw * raw, axis=0, keepdims=True)
            total = part if total is None else total + part
        edge_scale = lax.rsqrt(total / TRUNK_CHANNELS + EPSILON)
        for s in range(n_src):
            row0 = pl.multiple_of(ids_ref[s] * local_channels, 8)
            gain = gain_ref[pl.ds(row0, local_channels), :]
            for lo, scl in zip(range(0, token_positions, SLAB), core_scales):
                raw = cores[s][:, lo : lo + SLAB].astype(jnp.float32)
                act_ref[pl.ds(row0, local_channels), LANE + lo : LANE + lo + SLAB] = jax.nn.gelu(
                    raw * gain * scl
                )
            edge = jax.nn.gelu(edges[s][...].astype(jnp.float32) * gain * edge_scale)
            act_ref[pl.ds(row0, local_channels), LANE - border : LANE] = edge[:, :border]
            act_ref[pl.ds(row0, local_channels), LANE + token_positions : LANE + token_positions + border] = edge[:, border:]
        centre = kernel // 2
        for tap in range(kernel):
            copies[tap].wait()
            start = LANE + (tap - centre) * DILATION_STEP
            for lo in range(0, token_positions, MM_SLAB):
                rhs = act_ref[:, start + lo : start + lo + MM_SLAB].astype(jnp.bfloat16)
                term = jnp.dot(w_buf[tap], rhs, preferred_element_type=jnp.float32)
                if tap == 0:
                    acc_ref[:, lo : lo + MM_SLAB] = term
                else:
                    acc_ref[:, lo : lo + MM_SLAB] += term
        pool_rows = lax.broadcasted_iota(jnp.int32, (SLAB, SLAB // POOL), 0) // POOL
        pool_cols = lax.broadcasted_iota(jnp.int32, (SLAB, SLAB // POOL), 1)
        pool = jnp.where(pool_rows == pool_cols, 1.0 / POOL, 0.0).astype(jnp.bfloat16)
        for lo in range(0, token_positions, SLAB):
            out = (
                cores[0][:, lo : lo + SLAB].astype(jnp.float32)
                + acc_ref[:, lo : lo + SLAB]
                + bias_ref[...]
            ).astype(jnp.bfloat16)
            out_ref[:, lo : lo + SLAB] = out
            pooled_buf[:, lo // POOL : (lo + SLAB) // POOL] = jnp.dot(
                out, pool, preferred_element_type=jnp.float32
            )
        pooled = pooled_buf[...].astype(jnp.bfloat16)
        side_ref[: proj_ref.shape[0], :] = jnp.dot(
            proj_ref[...], pooled, preferred_element_type=jnp.float32
        )
        pooled_f = pooled.astype(jnp.float32)
        side_ref[proj_ref.shape[0] :, :] = jnp.sum(pooled_f * pooled_f, axis=0, keepdims=True)

    return body


def fused_conv(ids, gains, bias, own_proj, cores, edges, weights):
    n_src = len(cores)
    kernel, local_channels, all_channels = weights.shape
    token_positions = cores[0].shape[1]
    width = token_positions + 2 * LANE
    vmem = pl.BlockSpec(memory_space=pltpu.VMEM)
    return pl.pallas_call(
        conv_kernel(n_src, kernel, local_channels, token_positions),
        out_shape=(
            jax.ShapeDtypeStruct((local_channels, token_positions), jnp.bfloat16),
            jax.ShapeDtypeStruct((own_proj.shape[0] + 1, token_positions // POOL), jnp.float32),
        ),
        in_specs=[pl.BlockSpec(memory_space=pltpu.SMEM), vmem, vmem, vmem]
        + [vmem] * (2 * n_src)
        + [pl.BlockSpec(memory_space=pl.ANY)],
        out_specs=(vmem, vmem),
        scratch_shapes=[
            pltpu.VMEM((all_channels, width), jnp.float32),
            pltpu.VMEM((kernel, local_channels, all_channels), jnp.bfloat16),
            pltpu.VMEM((local_channels, token_positions), jnp.float32),
            pltpu.VMEM((local_channels, token_positions // POOL), jnp.float32),
            pltpu.SemaphoreType.DMA((kernel,)),
        ],
        compiler_params=pltpu.CompilerParams(vmem_limit_bytes=60 * 1024 * 1024),
    )(ids, gains, bias, own_proj, *cores, *edges, weights)


def per_device(
    trunk_in, conv_weight, conv_bias, norm_gain, pair_proj, pair_in, opm_weight, pair_bias
):
    local_channels = trunk_in.shape[0]
    token_positions = trunk_in.shape[1]
    kernel = conv_weight.shape[0]
    border_width = (kernel // 2) * DILATION_STEP
    n_col = lax.axis_size("col")
    row_index = lax.axis_index("row")
    col_index = lax.axis_index("col")

    n_row = lax.axis_size("row")
    from_left = lax.ppermute(
        trunk_in[:, token_positions - border_width :], "row", [(i, i + 1) for i in range(n_row - 1)]
    )
    from_right = lax.ppermute(
        trunk_in[:, :border_width], "row", [(i + 1, i) for i in range(n_row - 1)]
    )
    cores = [from_peer(trunk_in, "col", step) for step in range(1, n_col)]
    own_edges = jnp.concatenate([from_left, from_right], axis=1)
    edges = [from_peer(own_edges, "col", step) for step in range(1, n_col)]

    ids = jnp.stack([col_index] + [peer_of(col_index, step, n_col) for step in range(1, n_col)])
    ids = ids.astype(jnp.int32)
    own_proj = lax.dynamic_slice_in_dim(pair_proj, col_index * local_channels, local_channels, 1)
    trunk_out, packed = fused_conv(
        ids,
        norm_gain[:, None],
        conv_bias[:, None],
        own_proj,
        [trunk_in] + cores,
        [own_edges] + edges,
        conv_weight,
    )
    total = packed
    for step in range(1, n_col):
        total = total + from_peer(packed, "col", step)
    total = total.T
    side_width = total.shape[1] - 1
    projected = total[:, :side_width]
    sums = total[:, side_width]
    sides = (projected * lax.rsqrt(sums / TRUNK_CHANNELS + EPSILON)[:, None]).astype(jnp.bfloat16)
    row_side = sides[:, :OPM]
    collected = sides[:, OPM:]
    col_block = pair_in.shape[1]
    pooled_rows = row_side.shape[0]
    per_window = col_block * n_col // pooled_rows
    in_window = row_index % per_window
    for bit_num in range(per_window.bit_length() - 1):
        partner = partner_2(collected, "row", bit_num)
        upper_half = in_window // 2**bit_num % 2 == 1
        collected = jnp.where(
            upper_half,
            jnp.concatenate([partner, collected], axis=0),
            jnp.concatenate([collected, partner], axis=0),
        )
    own_cols = lax.dynamic_slice_in_dim(collected, col_index * col_block, col_block, 0)
    outer = (
        row_side.astype(jnp.float32)[:, None, :, None]
        * own_cols.astype(jnp.float32)[None, :, None, :]
    ).astype(jnp.bfloat16)
    outer = outer.reshape(pooled_rows * col_block, OPM * OPM)
    update = jnp.dot(outer, opm_weight, preferred_element_type=jnp.float32).reshape(pair_in.shape)
    pair_out = (pair_in.astype(jnp.float32) + update + pair_bias).astype(jnp.bfloat16)
    return (trunk_out, pair_out)


def solution(mesh):
    return jax.shard_map(
        per_device,
        mesh=mesh,
        in_specs=(
            P("col", "row"),
            P(None, "col", None),
            P("col"),
            P(),
            P(),
            P("row", "col", None),
            P(),
            P(),
        ),
        out_specs=(P("col", "row"), P("row", "col", None)),
        check_vma=False,
    )
```

```python
import jax
import jax.numpy as jnp
from jax import lax
from jax.sharding import PartitionSpec as P
from jax.experimental import pallas as pl
from jax.experimental.pallas import tpu as pltpu

TRUNK_CHANNELS = 1536
DILATION_STEP = 8
POOL = 16
OPM = 32

EPSILON = 1e-05


def with_halo(cells, sides, width):
    for axis, dim in sides:
        count = lax.axis_size(axis)
        ends = count - 1
        head = lax.slice_in_dim(cells, 0, width, axis=dim)
        tail = lax.slice_in_dim(cells, cells.shape[dim] - width, cells.shape[dim], axis=dim)
        cells = jnp.concatenate(
            [
                lax.ppermute(tail, axis, [(i, (i + 1) % count) for i in range(ends)]),
                cells,
                lax.ppermute(head, axis, [((i + 1) % count, i) for i in range(ends)]),
            ],
            axis=dim,
        )
    return cells


def partner_2(block, axis, bit):
    count = lax.axis_size(axis)
    route = []
    for low in range(count):
        high = low | 1 << bit
        if high != low and high < count:
            route += [(low, high), (high, low)]
    return lax.ppermute(block, axis, route)


def peer_of(index, step, count):
    if count & (count - 1) == 0:
        return index ^ step
    return (index + step) % count


def from_peer(block, axis, step):
    count = lax.axis_size(axis)
    if count & (count - 1) == 0:
        route = [(i, i ^ step) for i in range(count)]
    else:
        route = [((i + step) % count, i) for i in range(count)]
    return lax.ppermute(block, axis, route)


LANE = 128
SLAB = 256
MM_SLAB = 512


def conv_kernel(n_src, kernel, local_channels, token_positions):
    border = (kernel // 2) * DILATION_STEP

    def body(ids_ref, gain_ref, bias_ref, proj_ref, *refs):
        cores = refs[:n_src]
        edges = refs[n_src : 2 * n_src]
        w_hbm = refs[2 * n_src]
        out_ref, side_ref, act_ref, w_buf, acc_ref, pooled_buf, sems = refs[2 * n_src + 1 :]
        copies = [
            pltpu.make_async_copy(w_hbm.at[tap], w_buf.at[tap], sems.at[tap])
            for tap in range(kernel)
        ]
        for copy in copies:
            copy.start()
        core_scales = []
        for lo in range(0, token_positions, SLAB):
            total = None
            for s in range(n_src):
                raw = cores[s][:, lo : lo + SLAB].astype(jnp.float32)
                part = jnp.sum(raw * raw, axis=0, keepdims=True)
                total = part if total is None else total + part
            core_scales.append(lax.rsqrt(total / TRUNK_CHANNELS + EPSILON))
        total = None
        for s in range(n_src):
            raw = edges[s][...].astype(jnp.float32)
            part = jnp.sum(raw * raw, axis=0, keepdims=True)
            total = part if total is None else total + part
        edge_scale = lax.rsqrt(total / TRUNK_CHANNELS + EPSILON)
        for s in range(n_src):
            row0 = pl.multiple_of(ids_ref[s] * local_channels, 8)
            gain = gain_ref[pl.ds(row0, local_channels), :]
            for lo, scl in zip(range(0, token_positions, SLAB), core_scales):
                raw = cores[s][:, lo : lo + SLAB].astype(jnp.float32)
                act_ref[pl.ds(row0, local_channels), LANE + lo : LANE + lo + SLAB] = jax.nn.gelu(
                    raw * gain * scl
                )
            edge = jax.nn.gelu(edges[s][...].astype(jnp.float32) * gain * edge_scale)
            act_ref[pl.ds(row0, local_channels), LANE - border : LANE] = edge[:, :border]
            act_ref[pl.ds(row0, local_channels), LANE + token_positions : LANE + token_positions + border] = edge[:, border:]
        centre = kernel // 2
        for tap in range(kernel):
            copies[tap].wait()
            start = LANE + (tap - centre) * DILATION_STEP
            for lo in range(0, token_positions, MM_SLAB):
                rhs = act_ref[:, start + lo : start + lo + MM_SLAB].astype(jnp.bfloat16)
                term = jnp.dot(w_buf[tap], rhs, preferred_element_type=jnp.float32)
                if tap == 0:
                    acc_ref[:, lo : lo + MM_SLAB] = term
                else:
                    acc_ref[:, lo : lo + MM_SLAB] += term
        pool_rows = lax.broadcasted_iota(jnp.int32, (SLAB, SLAB // POOL), 0) // POOL
        pool_cols = lax.broadcasted_iota(jnp.int32, (SLAB, SLAB // POOL), 1)
        pool = jnp.where(pool_rows == pool_cols, 1.0 / POOL, 0.0).astype(jnp.bfloat16)
        for lo in range(0, token_positions, SLAB):
            out = (
                cores[0][:, lo : lo + SLAB].astype(jnp.float32)
                + acc_ref[:, lo : lo + SLAB]
                + bias_ref[...]
            ).astype(jnp.bfloat16)
            out_ref[:, lo : lo + SLAB] = out
            pooled_buf[:, lo // POOL : (lo + SLAB) // POOL] = jnp.dot(
                out, pool, preferred_element_type=jnp.float32
            )
        pooled = pooled_buf[...].astype(jnp.bfloat16)
        side_ref[: proj_ref.shape[0], :] = jnp.dot(
            proj_ref[...], pooled, preferred_element_type=jnp.float32
        )
        pooled_f = pooled.astype(jnp.float32)
        side_ref[proj_ref.shape[0] :, :] = jnp.sum(pooled_f * pooled_f, axis=0, keepdims=True)

    return body


def fused_conv(ids, gains, bias, own_proj, cores, edges, weights):
    n_src = len(cores)
    kernel, local_channels, all_channels = weights.shape
    token_positions = cores[0].shape[1]
    width = token_positions + 2 * LANE
    vmem = pl.BlockSpec(memory_space=pltpu.VMEM)
    return pl.pallas_call(
        conv_kernel(n_src, kernel, local_channels, token_positions),
        out_shape=(
            jax.ShapeDtypeStruct((local_channels, token_positions), jnp.bfloat16),
            jax.ShapeDtypeStruct((own_proj.shape[0] + 1, token_positions // POOL), jnp.float32),
        ),
        in_specs=[pl.BlockSpec(memory_space=pltpu.SMEM), vmem, vmem, vmem]
        + [vmem] * (2 * n_src)
        + [pl.BlockSpec(memory_space=pl.ANY)],
        out_specs=(vmem, vmem),
        scratch_shapes=[
            pltpu.VMEM((all_channels, width), jnp.float32),
            pltpu.VMEM((kernel, local_channels, all_channels), jnp.bfloat16),
            pltpu.VMEM((local_channels, token_positions), jnp.float32),
            pltpu.VMEM((local_channels, token_positions // POOL), jnp.float32),
            pltpu.SemaphoreType.DMA((kernel,)),
        ],
        compiler_params=pltpu.CompilerParams(vmem_limit_bytes=60 * 1024 * 1024),
    )(ids, gains, bias, own_proj, *cores, *edges, weights)


def per_device(
    trunk_in, conv_weight, conv_bias, norm_gain, pair_proj, pair_in, opm_weight, pair_bias
):
    local_channels = trunk_in.shape[0]
    token_positions = trunk_in.shape[1]
    kernel = conv_weight.shape[0]
    border_width = (kernel // 2) * DILATION_STEP
    n_col = lax.axis_size("col")
    row_index = lax.axis_index("row")
    col_index = lax.axis_index("col")

    n_row = lax.axis_size("row")
    from_left = lax.ppermute(
        trunk_in[:, token_positions - border_width :], "row", [(i, i + 1) for i in range(n_row - 1)]
    )
    from_right = lax.ppermute(
        trunk_in[:, :border_width], "row", [(i + 1, i) for i in range(n_row - 1)]
    )
    cores = [from_peer(trunk_in, "col", step) for step in range(1, n_col)]
    own_edges = jnp.concatenate([from_left, from_right], axis=1)
    edges = [from_peer(own_edges, "col", step) for step in range(1, n_col)]

    ids = jnp.stack([col_index] + [peer_of(col_index, step, n_col) for step in range(1, n_col)])
    ids = ids.astype(jnp.int32)
    own_proj = lax.dynamic_slice_in_dim(pair_proj, col_index * local_channels, local_channels, 1)
    trunk_out, packed = fused_conv(
        ids,
        norm_gain[:, None],
        conv_bias[:, None],
        own_proj,
        [trunk_in] + cores,
        [own_edges] + edges,
        conv_weight,
    )
    total = packed
    if n_col & (n_col - 1) == 0:
        bit = 1
        while bit < n_col:
            total = total + from_peer(total, "col", bit)
            bit *= 2
    else:
        for step in range(1, n_col):
            total = total + from_peer(packed, "col", step)
    total = total.T
    side_width = total.shape[1] - 1
    projected = total[:, :side_width]
    sums = total[:, side_width]
    sides = (projected * lax.rsqrt(sums / TRUNK_CHANNELS + EPSILON)[:, None]).astype(jnp.bfloat16)
    row_side = sides[:, :OPM]
    collected = sides[:, OPM:]
    col_block = pair_in.shape[1]
    pooled_rows = row_side.shape[0]
    per_window = col_block * n_col // pooled_rows
    in_window = row_index % per_window
    for bit_num in range(per_window.bit_length() - 1):
        partner = partner_2(collected, "row", bit_num)
        upper_half = in_window // 2**bit_num % 2 == 1
        collected = jnp.where(
            upper_half,
            jnp.concatenate([partner, collected], axis=0),
            jnp.concatenate([collected, partner], axis=0),
        )
    own_cols = lax.dynamic_slice_in_dim(collected, col_index * col_block, col_block, 0)
    outer = (
        row_side.astype(jnp.float32)[:, None, :, None]
        * own_cols.astype(jnp.float32)[None, :, None, :]
    ).astype(jnp.bfloat16)
    outer = outer.reshape(pooled_rows * col_block, OPM * OPM)
    update = jnp.dot(outer, opm_weight, preferred_element_type=jnp.float32).reshape(pair_in.shape)
    pair_out = (pair_in.astype(jnp.float32) + update + pair_bias).astype(jnp.bfloat16)
    return (trunk_out, pair_out)


def solution(mesh):
    return jax.shard_map(
        per_device,
        mesh=mesh,
        in_specs=(
            P("col", "row"),
            P(None, "col", None),
            P("col"),
            P(),
            P(),
            P("row", "col", None),
            P(),
            P(),
        ),
        out_specs=(P("col", "row"), P("row", "col", None)),
        check_vma=False,
    )
```

```python
import jax
import jax.numpy as jnp
from jax import lax
from jax.sharding import PartitionSpec as P
from jax.experimental import pallas as pl
from jax.experimental.pallas import tpu as pltpu

TRUNK_CHANNELS = 1536
DILATION_STEP = 8
POOL = 16
OPM = 32

EPSILON = 1e-05


def with_halo(cells, sides, width):
    for axis, dim in sides:
        count = lax.axis_size(axis)
        ends = count - 1
        head = lax.slice_in_dim(cells, 0, width, axis=dim)
        tail = lax.slice_in_dim(cells, cells.shape[dim] - width, cells.shape[dim], axis=dim)
        cells = jnp.concatenate(
            [
                lax.ppermute(tail, axis, [(i, (i + 1) % count) for i in range(ends)]),
                cells,
                lax.ppermute(head, axis, [((i + 1) % count, i) for i in range(ends)]),
            ],
            axis=dim,
        )
    return cells


def partner_2(block, axis, bit):
    count = lax.axis_size(axis)
    route = []
    for low in range(count):
        high = low | 1 << bit
        if high != low and high < count:
            route += [(low, high), (high, low)]
    return lax.ppermute(block, axis, route)


def peer_of(index, step, count):
    if count & (count - 1) == 0:
        return index ^ step
    return (index + step) % count


def from_peer(block, axis, step):
    count = lax.axis_size(axis)
    if count & (count - 1) == 0:
        route = [(i, i ^ step) for i in range(count)]
    else:
        route = [((i + step) % count, i) for i in range(count)]
    return lax.ppermute(block, axis, route)


LANE = 128
SLAB = 256
MM_SLAB = 512


def conv_kernel(n_src, kernel, local_channels, token_positions):
    border = (kernel // 2) * DILATION_STEP

    def body(ids_ref, gain_ref, bias_ref, proj_ref, *refs):
        cores = refs[:n_src]
        edges = refs[n_src : 2 * n_src]
        w_hbm = refs[2 * n_src]
        out_ref, side_ref, act_ref, w_buf, acc_ref, pooled_buf, sems = refs[2 * n_src + 1 :]
        copies = [
            pltpu.make_async_copy(w_hbm.at[tap], w_buf.at[tap], sems.at[tap])
            for tap in range(kernel)
        ]
        for copy in copies:
            copy.start()
        core_scales = []
        for lo in range(0, token_positions, SLAB):
            total = None
            for s in range(n_src):
                raw = cores[s][:, lo : lo + SLAB].astype(jnp.float32)
                part = jnp.sum(raw * raw, axis=0, keepdims=True)
                total = part if total is None else total + part
            core_scales.append(lax.rsqrt(total / TRUNK_CHANNELS + EPSILON))
        total = None
        for s in range(n_src):
            raw = edges[s][...].astype(jnp.float32)
            part = jnp.sum(raw * raw, axis=0, keepdims=True)
            total = part if total is None else total + part
        edge_scale = lax.rsqrt(total / TRUNK_CHANNELS + EPSILON)
        for s in range(n_src):
            row0 = pl.multiple_of(ids_ref[s] * local_channels, 8)
            gain = gain_ref[pl.ds(row0, local_channels), :]
            for lo, scl in zip(range(0, token_positions, SLAB), core_scales):
                raw = cores[s][:, lo : lo + SLAB].astype(jnp.float32)
                act_ref[pl.ds(row0, local_channels), LANE + lo : LANE + lo + SLAB] = jax.nn.gelu(
                    raw * gain * scl
                )
            edge = jax.nn.gelu(edges[s][...].astype(jnp.float32) * gain * edge_scale)
            act_ref[pl.ds(row0, local_channels), LANE - border : LANE] = edge[:, :border]
            act_ref[pl.ds(row0, local_channels), LANE + token_positions : LANE + token_positions + border] = edge[:, border:]
        centre = kernel // 2
        for tap in range(kernel):
            copies[tap].wait()
            start = LANE + (tap - centre) * DILATION_STEP
            for lo in range(0, token_positions, MM_SLAB):
                rhs = act_ref[:, start + lo : start + lo + MM_SLAB].astype(jnp.bfloat16)
                term = jnp.dot(w_buf[tap], rhs, preferred_element_type=jnp.float32)
                if tap == 0:
                    acc_ref[:, lo : lo + MM_SLAB] = term
                else:
                    acc_ref[:, lo : lo + MM_SLAB] += term
        pool_rows = lax.broadcasted_iota(jnp.int32, (SLAB, SLAB // POOL), 0) // POOL
        pool_cols = lax.broadcasted_iota(jnp.int32, (SLAB, SLAB // POOL), 1)
        pool = jnp.where(pool_rows == pool_cols, 1.0 / POOL, 0.0).astype(jnp.bfloat16)
        for lo in range(0, token_positions, SLAB):
            out = (
                cores[0][:, lo : lo + SLAB].astype(jnp.float32)
                + acc_ref[:, lo : lo + SLAB]
                + bias_ref[...]
            ).astype(jnp.bfloat16)
            out_ref[:, lo : lo + SLAB] = out
            pooled_buf[:, lo // POOL : (lo + SLAB) // POOL] = jnp.dot(
                out, pool, preferred_element_type=jnp.float32
            )
        pooled = pooled_buf[...].astype(jnp.bfloat16)
        side_ref[: proj_ref.shape[0], :] = jnp.dot(
            proj_ref[...], pooled, preferred_element_type=jnp.float32
        )
        pooled_f = pooled.astype(jnp.float32)
        side_ref[proj_ref.shape[0] :, :] = jnp.sum(pooled_f * pooled_f, axis=0, keepdims=True)

    return body


def fused_conv(ids, gains, bias, own_proj, cores, edges, weights):
    n_src = len(cores)
    kernel, local_channels, all_channels = weights.shape
    token_positions = cores[0].shape[1]
    width = token_positions + 2 * LANE
    vmem = pl.BlockSpec(memory_space=pltpu.VMEM)
    return pl.pallas_call(
        conv_kernel(n_src, kernel, local_channels, token_positions),
        out_shape=(
            jax.ShapeDtypeStruct((local_channels, token_positions), jnp.bfloat16),
            jax.ShapeDtypeStruct((own_proj.shape[0] + 1, token_positions // POOL), jnp.float32),
        ),
        in_specs=[pl.BlockSpec(memory_space=pltpu.SMEM), vmem, vmem, vmem]
        + [vmem] * (2 * n_src)
        + [pl.BlockSpec(memory_space=pl.ANY)],
        out_specs=(vmem, vmem),
        scratch_shapes=[
            pltpu.VMEM((all_channels, width), jnp.float32),
            pltpu.VMEM((kernel, local_channels, all_channels), jnp.bfloat16),
            pltpu.VMEM((local_channels, token_positions), jnp.float32),
            pltpu.VMEM((local_channels, token_positions // POOL), jnp.float32),
            pltpu.SemaphoreType.DMA((kernel,)),
        ],
        compiler_params=pltpu.CompilerParams(vmem_limit_bytes=60 * 1024 * 1024),
    )(ids, gains, bias, own_proj, *cores, *edges, weights)


def per_device(
    trunk_in, conv_weight, conv_bias, norm_gain, pair_proj, pair_in, opm_weight, pair_bias
):
    local_channels = trunk_in.shape[0]
    token_positions = trunk_in.shape[1]
    kernel = conv_weight.shape[0]
    border_width = (kernel // 2) * DILATION_STEP
    n_col = lax.axis_size("col")
    row_index = lax.axis_index("row")
    col_index = lax.axis_index("col")

    n_row = lax.axis_size("row")
    from_left = lax.ppermute(
        trunk_in[:, token_positions - border_width :], "row", [(i, i + 1) for i in range(n_row - 1)]
    )
    from_right = lax.ppermute(
        trunk_in[:, :border_width], "row", [(i + 1, i) for i in range(n_row - 1)]
    )
    cores = [from_peer(trunk_in, "col", step) for step in range(1, n_col)]
    own_edges = jnp.concatenate([from_left, from_right], axis=1)
    edges = [from_peer(own_edges, "col", step) for step in range(1, n_col)]

    ids = jnp.stack([col_index] + [peer_of(col_index, step, n_col) for step in range(1, n_col)])
    ids = ids.astype(jnp.int32)
    own_proj = lax.dynamic_slice_in_dim(pair_proj, col_index * local_channels, local_channels, 1)
    trunk_out, packed = fused_conv(
        ids,
        norm_gain[:, None],
        conv_bias[:, None],
        own_proj,
        [trunk_in] + cores,
        [own_edges] + edges,
        conv_weight,
    )
    total = packed
    for step in range(1, n_col):
        total = total + from_peer(packed, "col", step)
    total = total.T
    side_width = total.shape[1] - 1
    projected = total[:, :side_width]
    sums = total[:, side_width]
    sides = (projected * lax.rsqrt(sums / TRUNK_CHANNELS + EPSILON)[:, None]).astype(jnp.bfloat16)
    row_side = sides[:, :OPM]
    collected = sides[:, OPM:]
    col_block = pair_in.shape[1]
    pooled_rows = row_side.shape[0]
    per_window = col_block * n_col // pooled_rows
    in_window = row_index % per_window
    for bit_num in range(per_window.bit_length() - 1):
        partner = partner_2(collected, "row", bit_num)
        upper_half = in_window // 2**bit_num % 2 == 1
        collected = jnp.where(
            upper_half,
            jnp.concatenate([partner, collected], axis=0),
            jnp.concatenate([collected, partner], axis=0),
        )
    own_cols = lax.dynamic_slice_in_dim(collected, col_index * col_block, col_block, 0)
    per_row = opm_weight.reshape(OPM, OPM, opm_weight.shape[1])
    by_col = lax.dot_general(
        own_cols, per_row, (((1,), (1,)), ((), ())), preferred_element_type=jnp.float32
    )
    by_col = jnp.transpose(by_col, (1, 0, 2)).reshape(OPM, col_block * opm_weight.shape[1])
    update = jnp.dot(
        row_side.astype(jnp.float32),
        by_col,
        precision=lax.Precision.HIGHEST,
        preferred_element_type=jnp.float32,
    ).reshape(pair_in.shape)
    pair_out = (pair_in.astype(jnp.float32) + update + pair_bias).astype(jnp.bfloat16)
    return (trunk_out, pair_out)


def solution(mesh):
    return jax.shard_map(
        per_device,
        mesh=mesh,
        in_specs=(
            P("col", "row"),
            P(None, "col", None),
            P("col"),
            P(),
            P(),
            P("row", "col", None),
            P(),
            P(),
        ),
        out_specs=(P("col", "row"), P("row", "col", None)),
        check_vma=False,
    )
```

```python
import jax
import jax.numpy as jnp
from jax import lax
from jax.sharding import PartitionSpec as P
from jax.experimental import pallas as pl
from jax.experimental.pallas import tpu as pltpu

TRUNK_CHANNELS = 1536
DILATION_STEP = 8
POOL = 16
OPM = 32

EPSILON = 1e-05


def with_halo(cells, sides, width):
    for axis, dim in sides:
        count = lax.axis_size(axis)
        ends = count - 1
        head = lax.slice_in_dim(cells, 0, width, axis=dim)
        tail = lax.slice_in_dim(cells, cells.shape[dim] - width, cells.shape[dim], axis=dim)
        cells = jnp.concatenate(
            [
                lax.ppermute(tail, axis, [(i, (i + 1) % count) for i in range(ends)]),
                cells,
                lax.ppermute(head, axis, [((i + 1) % count, i) for i in range(ends)]),
            ],
            axis=dim,
        )
    return cells


def partner_2(block, axis, bit):
    count = lax.axis_size(axis)
    route = []
    for low in range(count):
        high = low | 1 << bit
        if high != low and high < count:
            route += [(low, high), (high, low)]
    return lax.ppermute(block, axis, route)


def peer_of(index, step, count):
    if count & (count - 1) == 0:
        return index ^ step
    return (index + step) % count


def from_peer(block, axis, step):
    count = lax.axis_size(axis)
    if count & (count - 1) == 0:
        route = [(i, i ^ step) for i in range(count)]
    else:
        route = [((i + step) % count, i) for i in range(count)]
    return lax.ppermute(block, axis, route)


LANE = 128
SLAB = 256
MM_SLAB = 1024


def conv_kernel(n_src, kernel, local_channels, token_positions):
    border = (kernel // 2) * DILATION_STEP

    def body(ids_ref, gain_ref, bias_ref, proj_ref, *refs):
        cores = refs[:n_src]
        edges = refs[n_src : 2 * n_src]
        w_hbm = refs[2 * n_src]
        out_ref, side_ref, act_ref, w_buf, acc_ref, pooled_buf, sems = refs[2 * n_src + 1 :]
        copies = [
            pltpu.make_async_copy(w_hbm.at[tap], w_buf.at[tap], sems.at[tap])
            for tap in range(kernel)
        ]
        for copy in copies:
            copy.start()
        core_scales = []
        for lo in range(0, token_positions, SLAB):
            total = None
            for s in range(n_src):
                raw = cores[s][:, lo : lo + SLAB].astype(jnp.float32)
                part = jnp.sum(raw * raw, axis=0, keepdims=True)
                total = part if total is None else total + part
            core_scales.append(lax.rsqrt(total / TRUNK_CHANNELS + EPSILON))
        total = None
        for s in range(n_src):
            raw = edges[s][...].astype(jnp.float32)
            part = jnp.sum(raw * raw, axis=0, keepdims=True)
            total = part if total is None else total + part
        edge_scale = lax.rsqrt(total / TRUNK_CHANNELS + EPSILON)
        for s in range(n_src):
            row0 = pl.multiple_of(ids_ref[s] * local_channels, 8)
            gain = gain_ref[pl.ds(row0, local_channels), :]
            for lo, scl in zip(range(0, token_positions, SLAB), core_scales):
                raw = cores[s][:, lo : lo + SLAB].astype(jnp.float32)
                act_ref[pl.ds(row0, local_channels), LANE + lo : LANE + lo + SLAB] = jax.nn.gelu(
                    raw * gain * scl
                )
            edge = jax.nn.gelu(edges[s][...].astype(jnp.float32) * gain * edge_scale)
            act_ref[pl.ds(row0, local_channels), LANE - border : LANE] = edge[:, :border]
            act_ref[pl.ds(row0, local_channels), LANE + token_positions : LANE + token_positions + border] = edge[:, border:]
        centre = kernel // 2
        for tap in range(kernel):
            copies[tap].wait()
            start = LANE + (tap - centre) * DILATION_STEP
            for lo in range(0, token_positions, MM_SLAB):
                rhs = act_ref[:, start + lo : start + lo + MM_SLAB].astype(jnp.bfloat16)
                term = jnp.dot(w_buf[tap], rhs, preferred_element_type=jnp.float32)
                if tap == 0:
                    acc_ref[:, lo : lo + MM_SLAB] = term
                else:
                    acc_ref[:, lo : lo + MM_SLAB] += term
        pool_rows = lax.broadcasted_iota(jnp.int32, (SLAB, SLAB // POOL), 0) // POOL
        pool_cols = lax.broadcasted_iota(jnp.int32, (SLAB, SLAB // POOL), 1)
        pool = jnp.where(pool_rows == pool_cols, 1.0 / POOL, 0.0).astype(jnp.bfloat16)
        for lo in range(0, token_positions, SLAB):
            out = (
                cores[0][:, lo : lo + SLAB].astype(jnp.float32)
                + acc_ref[:, lo : lo + SLAB]
                + bias_ref[...]
            ).astype(jnp.bfloat16)
            out_ref[:, lo : lo + SLAB] = out
            pooled_buf[:, lo // POOL : (lo + SLAB) // POOL] = jnp.dot(
                out, pool, preferred_element_type=jnp.float32
            )
        pooled = pooled_buf[...].astype(jnp.bfloat16)
        side_ref[: proj_ref.shape[0], :] = jnp.dot(
            proj_ref[...], pooled, preferred_element_type=jnp.float32
        )
        pooled_f = pooled.astype(jnp.float32)
        side_ref[proj_ref.shape[0] :, :] = jnp.sum(pooled_f * pooled_f, axis=0, keepdims=True)

    return body


def fused_conv(ids, gains, bias, own_proj, cores, edges, weights):
    n_src = len(cores)
    kernel, local_channels, all_channels = weights.shape
    token_positions = cores[0].shape[1]
    width = token_positions + 2 * LANE
    vmem = pl.BlockSpec(memory_space=pltpu.VMEM)
    return pl.pallas_call(
        conv_kernel(n_src, kernel, local_channels, token_positions),
        out_shape=(
            jax.ShapeDtypeStruct((local_channels, token_positions), jnp.bfloat16),
            jax.ShapeDtypeStruct((own_proj.shape[0] + 1, token_positions // POOL), jnp.float32),
        ),
        in_specs=[pl.BlockSpec(memory_space=pltpu.SMEM), vmem, vmem, vmem]
        + [vmem] * (2 * n_src)
        + [pl.BlockSpec(memory_space=pl.ANY)],
        out_specs=(vmem, vmem),
        scratch_shapes=[
            pltpu.VMEM((all_channels, width), jnp.float32),
            pltpu.VMEM((kernel, local_channels, all_channels), jnp.bfloat16),
            pltpu.VMEM((local_channels, token_positions), jnp.float32),
            pltpu.VMEM((local_channels, token_positions // POOL), jnp.float32),
            pltpu.SemaphoreType.DMA((kernel,)),
        ],
        compiler_params=pltpu.CompilerParams(vmem_limit_bytes=60 * 1024 * 1024),
    )(ids, gains, bias, own_proj, *cores, *edges, weights)


def per_device(
    trunk_in, conv_weight, conv_bias, norm_gain, pair_proj, pair_in, opm_weight, pair_bias
):
    local_channels = trunk_in.shape[0]
    token_positions = trunk_in.shape[1]
    kernel = conv_weight.shape[0]
    border_width = (kernel // 2) * DILATION_STEP
    n_col = lax.axis_size("col")
    row_index = lax.axis_index("row")
    col_index = lax.axis_index("col")

    n_row = lax.axis_size("row")
    from_left = lax.ppermute(
        trunk_in[:, token_positions - border_width :], "row", [(i, i + 1) for i in range(n_row - 1)]
    )
    from_right = lax.ppermute(
        trunk_in[:, :border_width], "row", [(i + 1, i) for i in range(n_row - 1)]
    )
    cores = [from_peer(trunk_in, "col", step) for step in range(1, n_col)]
    own_edges = jnp.concatenate([from_left, from_right], axis=1)
    edges = [from_peer(own_edges, "col", step) for step in range(1, n_col)]

    ids = jnp.stack([col_index] + [peer_of(col_index, step, n_col) for step in range(1, n_col)])
    ids = ids.astype(jnp.int32)
    own_proj = lax.dynamic_slice_in_dim(pair_proj, col_index * local_channels, local_channels, 1)
    trunk_out, packed = fused_conv(
        ids,
        norm_gain[:, None],
        conv_bias[:, None],
        own_proj,
        [trunk_in] + cores,
        [own_edges] + edges,
        conv_weight,
    )
    total = packed
    for step in range(1, n_col):
        total = total + from_peer(packed, "col", step)
    total = total.T
    side_width = total.shape[1] - 1
    projected = total[:, :side_width]
    sums = total[:, side_width]
    sides = (projected * lax.rsqrt(sums / TRUNK_CHANNELS + EPSILON)[:, None]).astype(jnp.bfloat16)
    row_side = sides[:, :OPM]
    collected = sides[:, OPM:]
    col_block = pair_in.shape[1]
    pooled_rows = row_side.shape[0]
    per_window = col_block * n_col // pooled_rows
    in_window = row_index % per_window
    for bit_num in range(per_window.bit_length() - 1):
        partner = partner_2(collected, "row", bit_num)
        upper_half = in_window // 2**bit_num % 2 == 1
        collected = jnp.where(
            upper_half,
            jnp.concatenate([partner, collected], axis=0),
            jnp.concatenate([collected, partner], axis=0),
        )
    own_cols = lax.dynamic_slice_in_dim(collected, col_index * col_block, col_block, 0)
    outer = (
        row_side.astype(jnp.float32)[:, None, :, None]
        * own_cols.astype(jnp.float32)[None, :, None, :]
    ).astype(jnp.bfloat16)
    outer = outer.reshape(pooled_rows * col_block, OPM * OPM)
    update = jnp.dot(outer, opm_weight, preferred_element_type=jnp.float32).reshape(pair_in.shape)
    pair_out = (pair_in.astype(jnp.float32) + update + pair_bias).astype(jnp.bfloat16)
    return (trunk_out, pair_out)


def solution(mesh):
    return jax.shard_map(
        per_device,
        mesh=mesh,
        in_specs=(
            P("col", "row"),
            P(None, "col", None),
            P("col"),
            P(),
            P(),
            P("row", "col", None),
            P(),
            P(),
        ),
        out_specs=(P("col", "row"), P("row", "col", None)),
        check_vma=False,
    )
```

```python
import jax
import jax.numpy as jnp
from jax import lax
from jax.sharding import PartitionSpec as P
from jax.experimental import pallas as pl
from jax.experimental.pallas import tpu as pltpu

TRUNK_CHANNELS = 1536
DILATION_STEP = 8
POOL = 16
OPM = 32

EPSILON = 1e-05


def with_halo(cells, sides, width):
    for axis, dim in sides:
        count = lax.axis_size(axis)
        ends = count - 1
        head = lax.slice_in_dim(cells, 0, width, axis=dim)
        tail = lax.slice_in_dim(cells, cells.shape[dim] - width, cells.shape[dim], axis=dim)
        cells = jnp.concatenate(
            [
                lax.ppermute(tail, axis, [(i, (i + 1) % count) for i in range(ends)]),
                cells,
                lax.ppermute(head, axis, [((i + 1) % count, i) for i in range(ends)]),
            ],
            axis=dim,
        )
    return cells


def partner_2(block, axis, bit):
    count = lax.axis_size(axis)
    route = []
    for low in range(count):
        high = low | 1 << bit
        if high != low and high < count:
            route += [(low, high), (high, low)]
    return lax.ppermute(block, axis, route)


def peer_of(index, step, count):
    if count & (count - 1) == 0:
        return index ^ step
    return (index + step) % count


def from_peer(block, axis, step):
    count = lax.axis_size(axis)
    if count & (count - 1) == 0:
        route = [(i, i ^ step) for i in range(count)]
    else:
        route = [((i + step) % count, i) for i in range(count)]
    return lax.ppermute(block, axis, route)


def gelu_tanh(x):
    u = 0.7978845608028654 * (x + 0.044715 * (x * x * x))
    return x / (1.0 + jnp.exp(-2.0 * u))


LANE = 128
SLAB = 256
MM_SLAB = 512


def conv_kernel(n_src, kernel, local_channels, token_positions):
    border = (kernel // 2) * DILATION_STEP

    def body(ids_ref, gain_ref, bias_ref, proj_ref, *refs):
        cores = refs[:n_src]
        edges = refs[n_src : 2 * n_src]
        w_hbm = refs[2 * n_src]
        out_ref, side_ref, act_ref, w_buf, acc_ref, pooled_buf, sems = refs[2 * n_src + 1 :]
        copies = [
            pltpu.make_async_copy(w_hbm.at[tap], w_buf.at[tap], sems.at[tap])
            for tap in range(kernel)
        ]
        for copy in copies:
            copy.start()
        core_scales = []
        for lo in range(0, token_positions, SLAB):
            total = None
            for s in range(n_src):
                raw = cores[s][:, lo : lo + SLAB].astype(jnp.float32)
                part = jnp.sum(raw * raw, axis=0, keepdims=True)
                total = part if total is None else total + part
            core_scales.append(lax.rsqrt(total / TRUNK_CHANNELS + EPSILON))
        total = None
        for s in range(n_src):
            raw = edges[s][...].astype(jnp.float32)
            part = jnp.sum(raw * raw, axis=0, keepdims=True)
            total = part if total is None else total + part
        edge_scale = lax.rsqrt(total / TRUNK_CHANNELS + EPSILON)
        for s in range(n_src):
            row0 = pl.multiple_of(ids_ref[s] * local_channels, 8)
            gain = gain_ref[pl.ds(row0, local_channels), :]
            for lo, scl in zip(range(0, token_positions, SLAB), core_scales):
                raw = cores[s][:, lo : lo + SLAB].astype(jnp.float32)
                act_ref[pl.ds(row0, local_channels), LANE + lo : LANE + lo + SLAB] = gelu_tanh(
                    raw * gain * scl
                )
            edge = gelu_tanh(edges[s][...].astype(jnp.float32) * gain * edge_scale)
            act_ref[pl.ds(row0, local_channels), LANE - border : LANE] = edge[:, :border]
            act_ref[pl.ds(row0, local_channels), LANE + token_positions : LANE + token_positions + border] = edge[:, border:]
        centre = kernel // 2
        for tap in range(kernel):
            copies[tap].wait()
            start = LANE + (tap - centre) * DILATION_STEP
            for lo in range(0, token_positions, MM_SLAB):
                rhs = act_ref[:, start + lo : start + lo + MM_SLAB].astype(jnp.bfloat16)
                term = jnp.dot(w_buf[tap], rhs, preferred_element_type=jnp.float32)
                if tap == 0:
                    acc_ref[:, lo : lo + MM_SLAB] = term
                else:
                    acc_ref[:, lo : lo + MM_SLAB] += term
        pool_rows = lax.broadcasted_iota(jnp.int32, (SLAB, SLAB // POOL), 0) // POOL
        pool_cols = lax.broadcasted_iota(jnp.int32, (SLAB, SLAB // POOL), 1)
        pool = jnp.where(pool_rows == pool_cols, 1.0 / POOL, 0.0).astype(jnp.bfloat16)
        for lo in range(0, token_positions, SLAB):
            out = (
                cores[0][:, lo : lo + SLAB].astype(jnp.float32)
                + acc_ref[:, lo : lo + SLAB]
                + bias_ref[...]
            ).astype(jnp.bfloat16)
            out_ref[:, lo : lo + SLAB] = out
            pooled_buf[:, lo // POOL : (lo + SLAB) // POOL] = jnp.dot(
                out, pool, preferred_element_type=jnp.float32
            )
        pooled = pooled_buf[...].astype(jnp.bfloat16)
        side_ref[: proj_ref.shape[0], :] = jnp.dot(
            proj_ref[...], pooled, preferred_element_type=jnp.float32
        )
        pooled_f = pooled.astype(jnp.float32)
        side_ref[proj_ref.shape[0] :, :] = jnp.sum(pooled_f * pooled_f, axis=0, keepdims=True)

    return body


def fused_conv(ids, gains, bias, own_proj, cores, edges, weights):
    n_src = len(cores)
    kernel, local_channels, all_channels = weights.shape
    token_positions = cores[0].shape[1]
    width = token_positions + 2 * LANE
    vmem = pl.BlockSpec(memory_space=pltpu.VMEM)
    return pl.pallas_call(
        conv_kernel(n_src, kernel, local_channels, token_positions),
        out_shape=(
            jax.ShapeDtypeStruct((local_channels, token_positions), jnp.bfloat16),
            jax.ShapeDtypeStruct((own_proj.shape[0] + 1, token_positions // POOL), jnp.float32),
        ),
        in_specs=[pl.BlockSpec(memory_space=pltpu.SMEM), vmem, vmem, vmem]
        + [vmem] * (2 * n_src)
        + [pl.BlockSpec(memory_space=pl.ANY)],
        out_specs=(vmem, vmem),
        scratch_shapes=[
            pltpu.VMEM((all_channels, width), jnp.float32),
            pltpu.VMEM((kernel, local_channels, all_channels), jnp.bfloat16),
            pltpu.VMEM((local_channels, token_positions), jnp.float32),
            pltpu.VMEM((local_channels, token_positions // POOL), jnp.float32),
            pltpu.SemaphoreType.DMA((kernel,)),
        ],
        compiler_params=pltpu.CompilerParams(vmem_limit_bytes=60 * 1024 * 1024),
    )(ids, gains, bias, own_proj, *cores, *edges, weights)


def per_device(
    trunk_in, conv_weight, conv_bias, norm_gain, pair_proj, pair_in, opm_weight, pair_bias
):
    local_channels = trunk_in.shape[0]
    token_positions = trunk_in.shape[1]
    kernel = conv_weight.shape[0]
    border_width = (kernel // 2) * DILATION_STEP
    n_col = lax.axis_size("col")
    row_index = lax.axis_index("row")
    col_index = lax.axis_index("col")

    n_row = lax.axis_size("row")
    from_left = lax.ppermute(
        trunk_in[:, token_positions - border_width :], "row", [(i, i + 1) for i in range(n_row - 1)]
    )
    from_right = lax.ppermute(
        trunk_in[:, :border_width], "row", [(i + 1, i) for i in range(n_row - 1)]
    )
    cores = [from_peer(trunk_in, "col", step) for step in range(1, n_col)]
    own_edges = jnp.concatenate([from_left, from_right], axis=1)
    edges = [from_peer(own_edges, "col", step) for step in range(1, n_col)]

    ids = jnp.stack([col_index] + [peer_of(col_index, step, n_col) for step in range(1, n_col)])
    ids = ids.astype(jnp.int32)
    own_proj = lax.dynamic_slice_in_dim(pair_proj, col_index * local_channels, local_channels, 1)
    trunk_out, packed = fused_conv(
        ids,
        norm_gain[:, None],
        conv_bias[:, None],
        own_proj,
        [trunk_in] + cores,
        [own_edges] + edges,
        conv_weight,
    )
    total = packed
    for step in range(1, n_col):
        total = total + from_peer(packed, "col", step)
    total = total.T
    side_width = total.shape[1] - 1
    projected = total[:, :side_width]
    sums = total[:, side_width]
    sides = (projected * lax.rsqrt(sums / TRUNK_CHANNELS + EPSILON)[:, None]).astype(jnp.bfloat16)
    row_side = sides[:, :OPM]
    collected = sides[:, OPM:]
    col_block = pair_in.shape[1]
    pooled_rows = row_side.shape[0]
    per_window = col_block * n_col // pooled_rows
    in_window = row_index % per_window
    for bit_num in range(per_window.bit_length() - 1):
        partner = partner_2(collected, "row", bit_num)
        upper_half = in_window // 2**bit_num % 2 == 1
        collected = jnp.where(
            upper_half,
            jnp.concatenate([partner, collected], axis=0),
            jnp.concatenate([collected, partner], axis=0),
        )
    own_cols = lax.dynamic_slice_in_dim(collected, col_index * col_block, col_block, 0)
    outer = (
        row_side.astype(jnp.float32)[:, None, :, None]
        * own_cols.astype(jnp.float32)[None, :, None, :]
    ).astype(jnp.bfloat16)
    outer = outer.reshape(pooled_rows * col_block, OPM * OPM)
    update = jnp.dot(outer, opm_weight, preferred_element_type=jnp.float32).reshape(pair_in.shape)
    pair_out = (pair_in.astype(jnp.float32) + update + pair_bias).astype(jnp.bfloat16)
    return (trunk_out, pair_out)


def solution(mesh):
    return jax.shard_map(
        per_device,
        mesh=mesh,
        in_specs=(
            P("col", "row"),
            P(None, "col", None),
            P("col"),
            P(),
            P(),
            P("row", "col", None),
            P(),
            P(),
        ),
        out_specs=(P("col", "row"), P("row", "col", None)),
        check_vma=False,
    )
```

```python
import jax
import jax.numpy as jnp
from jax import lax
from jax.sharding import PartitionSpec as P
from jax.experimental import pallas as pl
from jax.experimental.pallas import tpu as pltpu

TRUNK_CHANNELS = 1536
DILATION_STEP = 8
POOL = 16
OPM = 32

EPSILON = 1e-05


def with_halo(cells, sides, width):
    for axis, dim in sides:
        count = lax.axis_size(axis)
        ends = count - 1
        head = lax.slice_in_dim(cells, 0, width, axis=dim)
        tail = lax.slice_in_dim(cells, cells.shape[dim] - width, cells.shape[dim], axis=dim)
        cells = jnp.concatenate(
            [
                lax.ppermute(tail, axis, [(i, (i + 1) % count) for i in range(ends)]),
                cells,
                lax.ppermute(head, axis, [((i + 1) % count, i) for i in range(ends)]),
            ],
            axis=dim,
        )
    return cells


def partner_2(block, axis, bit):
    count = lax.axis_size(axis)
    route = []
    for low in range(count):
        high = low | 1 << bit
        if high != low and high < count:
            route += [(low, high), (high, low)]
    return lax.ppermute(block, axis, route)


def peer_of(index, step, count):
    if count & (count - 1) == 0:
        return index ^ step
    return (index + step) % count


def from_peer(block, axis, step):
    count = lax.axis_size(axis)
    if count & (count - 1) == 0:
        route = [(i, i ^ step) for i in range(count)]
    else:
        route = [((i + step) % count, i) for i in range(count)]
    return lax.ppermute(block, axis, route)


LANE = 128
SLAB = 512
MM_SLAB = 512


def conv_kernel(n_src, kernel, local_channels, token_positions):
    border = (kernel // 2) * DILATION_STEP

    def body(ids_ref, gain_ref, bias_ref, proj_ref, *refs):
        cores = refs[:n_src]
        edges = refs[n_src : 2 * n_src]
        w_hbm = refs[2 * n_src]
        out_ref, side_ref, act_ref, w_buf, acc_ref, pooled_buf, sems = refs[2 * n_src + 1 :]
        copies = [
            pltpu.make_async_copy(w_hbm.at[tap], w_buf.at[tap], sems.at[tap])
            for tap in range(kernel)
        ]
        for copy in copies:
            copy.start()
        core_scales = []
        for lo in range(0, token_positions, SLAB):
            total = None
            for s in range(n_src):
                raw = cores[s][:, lo : lo + SLAB].astype(jnp.float32)
                part = jnp.sum(raw * raw, axis=0, keepdims=True)
                total = part if total is None else total + part
            core_scales.append(lax.rsqrt(total / TRUNK_CHANNELS + EPSILON))
        total = None
        for s in range(n_src):
            raw = edges[s][...].astype(jnp.float32)
            part = jnp.sum(raw * raw, axis=0, keepdims=True)
            total = part if total is None else total + part
        edge_scale = lax.rsqrt(total / TRUNK_CHANNELS + EPSILON)
        for s in range(n_src):
            row0 = pl.multiple_of(ids_ref[s] * local_channels, 8)
            gain = gain_ref[pl.ds(row0, local_channels), :]
            for lo, scl in zip(range(0, token_positions, SLAB), core_scales):
                raw = cores[s][:, lo : lo + SLAB].astype(jnp.float32)
                act_ref[pl.ds(row0, local_channels), LANE + lo : LANE + lo + SLAB] = jax.nn.gelu(
                    raw * gain * scl
                )
            edge = jax.nn.gelu(edges[s][...].astype(jnp.float32) * gain * edge_scale)
            act_ref[pl.ds(row0, local_channels), LANE - border : LANE] = edge[:, :border]
            act_ref[pl.ds(row0, local_channels), LANE + token_positions : LANE + token_positions + border] = edge[:, border:]
        centre = kernel // 2
        for tap in range(kernel):
            copies[tap].wait()
            start = LANE + (tap - centre) * DILATION_STEP
            for lo in range(0, token_positions, MM_SLAB):
                rhs = act_ref[:, start + lo : start + lo + MM_SLAB].astype(jnp.bfloat16)
                term = jnp.dot(w_buf[tap], rhs, preferred_element_type=jnp.float32)
                if tap == 0:
                    acc_ref[:, lo : lo + MM_SLAB] = term
                else:
                    acc_ref[:, lo : lo + MM_SLAB] += term
        pool_rows = lax.broadcasted_iota(jnp.int32, (SLAB, SLAB // POOL), 0) // POOL
        pool_cols = lax.broadcasted_iota(jnp.int32, (SLAB, SLAB // POOL), 1)
        pool = jnp.where(pool_rows == pool_cols, 1.0 / POOL, 0.0).astype(jnp.bfloat16)
        for lo in range(0, token_positions, SLAB):
            out = (
                cores[0][:, lo : lo + SLAB].astype(jnp.float32)
                + acc_ref[:, lo : lo + SLAB]
                + bias_ref[...]
            ).astype(jnp.bfloat16)
            out_ref[:, lo : lo + SLAB] = out
            pooled_buf[:, lo // POOL : (lo + SLAB) // POOL] = jnp.dot(
                out, pool, preferred_element_type=jnp.float32
            )
        pooled = pooled_buf[...].astype(jnp.bfloat16)
        side_ref[: proj_ref.shape[0], :] = jnp.dot(
            proj_ref[...], pooled, preferred_element_type=jnp.float32
        )
        pooled_f = pooled.astype(jnp.float32)
        side_ref[proj_ref.shape[0] :, :] = jnp.sum(pooled_f * pooled_f, axis=0, keepdims=True)

    return body


def fused_conv(ids, gains, bias, own_proj, cores, edges, weights):
    n_src = len(cores)
    kernel, local_channels, all_channels = weights.shape
    token_positions = cores[0].shape[1]
    width = token_positions + 2 * LANE
    vmem = pl.BlockSpec(memory_space=pltpu.VMEM)
    return pl.pallas_call(
        conv_kernel(n_src, kernel, local_channels, token_positions),
        out_shape=(
            jax.ShapeDtypeStruct((local_channels, token_positions), jnp.bfloat16),
            jax.ShapeDtypeStruct((own_proj.shape[0] + 1, token_positions // POOL), jnp.float32),
        ),
        in_specs=[pl.BlockSpec(memory_space=pltpu.SMEM), vmem, vmem, vmem]
        + [vmem] * (2 * n_src)
        + [pl.BlockSpec(memory_space=pl.ANY)],
        out_specs=(vmem, vmem),
        scratch_shapes=[
            pltpu.VMEM((all_channels, width), jnp.float32),
            pltpu.VMEM((kernel, local_channels, all_channels), jnp.bfloat16),
            pltpu.VMEM((local_channels, token_positions), jnp.float32),
            pltpu.VMEM((local_channels, token_positions // POOL), jnp.float32),
            pltpu.SemaphoreType.DMA((kernel,)),
        ],
        compiler_params=pltpu.CompilerParams(vmem_limit_bytes=60 * 1024 * 1024),
    )(ids, gains, bias, own_proj, *cores, *edges, weights)


def per_device(
    trunk_in, conv_weight, conv_bias, norm_gain, pair_proj, pair_in, opm_weight, pair_bias
):
    local_channels = trunk_in.shape[0]
    token_positions = trunk_in.shape[1]
    kernel = conv_weight.shape[0]
    border_width = (kernel // 2) * DILATION_STEP
    n_col = lax.axis_size("col")
    row_index = lax.axis_index("row")
    col_index = lax.axis_index("col")

    n_row = lax.axis_size("row")
    from_left = lax.ppermute(
        trunk_in[:, token_positions - border_width :], "row", [(i, i + 1) for i in range(n_row - 1)]
    )
    from_right = lax.ppermute(
        trunk_in[:, :border_width], "row", [(i + 1, i) for i in range(n_row - 1)]
    )
    cores = [from_peer(trunk_in, "col", step) for step in range(1, n_col)]
    own_edges = jnp.concatenate([from_left, from_right], axis=1)
    edges = [from_peer(own_edges, "col", step) for step in range(1, n_col)]

    ids = jnp.stack([col_index] + [peer_of(col_index, step, n_col) for step in range(1, n_col)])
    ids = ids.astype(jnp.int32)
    own_proj = lax.dynamic_slice_in_dim(pair_proj, col_index * local_channels, local_channels, 1)
    trunk_out, packed = fused_conv(
        ids,
        norm_gain[:, None],
        conv_bias[:, None],
        own_proj,
        [trunk_in] + cores,
        [own_edges] + edges,
        conv_weight,
    )
    total = packed
    for step in range(1, n_col):
        total = total + from_peer(packed, "col", step)
    total = total.T
    side_width = total.shape[1] - 1
    projected = total[:, :side_width]
    sums = total[:, side_width]
    sides = (projected * lax.rsqrt(sums / TRUNK_CHANNELS + EPSILON)[:, None]).astype(jnp.bfloat16)
    row_side = sides[:, :OPM]
    collected = sides[:, OPM:]
    col_block = pair_in.shape[1]
    pooled_rows = row_side.shape[0]
    per_window = col_block * n_col // pooled_rows
    in_window = row_index % per_window
    for bit_num in range(per_window.bit_length() - 1):
        partner = partner_2(collected, "row", bit_num)
        upper_half = in_window // 2**bit_num % 2 == 1
        collected = jnp.where(
            upper_half,
            jnp.concatenate([partner, collected], axis=0),
            jnp.concatenate([collected, partner], axis=0),
        )
    own_cols = lax.dynamic_slice_in_dim(collected, col_index * col_block, col_block, 0)
    outer = (
        row_side.astype(jnp.float32)[:, None, :, None]
        * own_cols.astype(jnp.float32)[None, :, None, :]
    ).astype(jnp.bfloat16)
    outer = outer.reshape(pooled_rows * col_block, OPM * OPM)
    update = jnp.dot(outer, opm_weight, preferred_element_type=jnp.float32).reshape(pair_in.shape)
    pair_out = (pair_in.astype(jnp.float32) + update + pair_bias).astype(jnp.bfloat16)
    return (trunk_out, pair_out)


def solution(mesh):
    return jax.shard_map(
        per_device,
        mesh=mesh,
        in_specs=(
            P("col", "row"),
            P(None, "col", None),
            P("col"),
            P(),
            P(),
            P("row", "col", None),
            P(),
            P(),
        ),
        out_specs=(P("col", "row"), P("row", "col", None)),
        check_vma=False,
    )
```
